1024 devices in a mesh: calls: 32 (over y_hi, z, core), ctx: 32 (over x, y_lo).
Axes of the slice: x: 8, y: 8 (y_hi: 2, y_lo: 4; y = y_hi * 4 + y_lo), z: 8, core: 2. Of those that a mesh axis runs over, the one named last changes fastest.
Arguments:
- frames_in: bfloat16 [32, 4096, 1024], P('calls', 'ctx'), may hold values from -12 to 12
- w_qkv: bfloat16 [1024, 1536], replicated, may hold values from -1 to 1
- out_grad: bfloat16 [32, 4096, 512], P('calls', 'ctx'), may hold values from -6 to 6
- lengths: int32 [32], P('calls'), may hold values from 2048 to 4096, as said below
Outputs:
- context: bfloat16 [32, 4096, 512], P('calls', 'ctx')
- in_grad: bfloat16 [32, 4096, 1024], P('calls', 'ctx')
- weight_grad: float32 [1024, 1536], P('calls', 'ctx')
The draws below stay inside these ranges and needn't reach their ends.
Inputs may be any that keep to these rules, and one draw needn't show every extreme that they name: Frames at and beyond lengths[c] are padding of call c; some call has all 4096 frames valid.
All inputs are finite; a program needn't handle non-finite values.
Results may differ from the reference program's by a relative error of at most 0.012.
The reference program's roundings to bfloat16 on the way count: a program that leaves them out, or rounds other values in their place, can miss the bound.
Values may be sent and summed in bfloat16 or wider, within the bound.
No kernel may reach another device: no remote copies, remote signals or barrier semaphores. Data moves between devices by JAX's collectives and lax.ppermute only.
A program may use at most 64 MiB of HBM per device.

```python
import math
import jax
import jax.numpy as jnp
from jax import lax

D = 1024
HEADS = 4
WIN = 128
FRAMES_DEV = 128
HD = 512
FRAMES = 4096
CALLS = 32


def draw_lengths(key, part):
    key_draw, key_pick = jax.random.split(jax.random.fold_in(key, 17))
    lengths_drawn = jax.random.randint(key_draw, (CALLS,), FRAMES // 2, FRAMES + 1)
    picked = jax.random.randint(key_pick, (), 0, CALLS)
    return jnp.where(jnp.arange(CALLS) == picked, FRAMES, lengths_drawn).astype(jnp.int32)


def draw_w_qkv(key, part):
    key_query, key_other, key_value = jax.random.split(jax.random.fold_in(key, 31), 3)
    w_query = jnp.clip(jax.random.normal(key_query, (D, HD), jnp.float32), -4.0, 4.0)
    w_key = jnp.clip(jax.random.normal(key_other, (D, HD), jnp.float32), -4.0, 4.0)
    w_value = jnp.clip(jax.random.normal(key_value, (D, HD), jnp.float32), -4.0, 4.0)
    return (jnp.concatenate([w_query, w_key, w_value], axis=1) / math.sqrt(D)).astype(jnp.bfloat16)


def draw_frames_in(key, part):
    key_base, key_perm = jax.random.split(jax.random.fold_in(key, 29), 2)
    order = jax.random.permutation(key_perm, CALLS)
    frame_block = jnp.arange(FRAMES, dtype=jnp.int32) // FRAMES_DEV
    column_owner = jnp.arange(D, dtype=jnp.int32) // (D // CALLS)
    boost = jnp.where(column_owner[None, :] == order[frame_block % CALLS][:, None], 3.0, 1.0)
    normal = jnp.clip(jax.random.normal(key_base, (CALLS, FRAMES, D), jnp.float32), -4.0, 4.0)
    result = normal * boost[None]
    return result.astype(jnp.bfloat16)


def level_of(own_key, dims, pieces, low, largest):
    def one(dim, shards_of):
        heights = jax.random.uniform(jax.random.fold_in(jax.random.fold_in(own_key, 6), dim), (shards_of,), jnp.float32, low / len(pieces), largest / len(pieces))
        return jnp.repeat(jnp.exp(heights), dims[dim] // shards_of).reshape((-1,) + (1,) * (len(dims) - dim - 1))

    loudness = one(*pieces[0])
    for cut in pieces[1:]:
        loudness = loudness * one(*cut)
    return loudness


def gaussian(own_key, shape, spread, most, cuts=(), kind=jnp.bfloat16):
    gain = level_of(own_key, shape, cuts, -0.22, 0.18) if cuts else 1.0
    values = jax.random.normal(own_key, shape, jnp.float32) * spread * gain
    return jnp.minimum(jnp.maximum(values, -most), most).astype(kind)


def setup_inputs(seed: int = 0) -> dict:
    splits = jax.random.split(jax.random.key(seed), 5)
    frames_in = draw_frames_in(jax.random.fold_in(splits[4], 71), 0)
    w_qkv = draw_w_qkv(jax.random.fold_in(splits[4], 71), 0)
    out_grad = gaussian(splits[2], (CALLS, FRAMES, HD), 1.0, 6.0, ((0, 32), (1, 32)))
    lengths = draw_lengths(jax.random.fold_in(splits[4], 71), 0)
    return dict(frames_in=frames_in, w_qkv=w_qkv, out_grad=out_grad, lengths=lengths)


def band_mask(query_pos, key_pos, length_now):
    gap = jnp.abs(query_pos[:, None] - key_pos[None, :])
    inside = (gap <= WIN) & (key_pos[None, :] >= 0) & (key_pos[None, :] < length_now)
    return inside | (query_pos[:, None] == key_pos[None, :])

def attend(queries, key_value, cotangent, allowed, living):
    frame_count, inner_width = queries.shape
    head_size = inner_width // HEADS
    key_span = key_value.shape[0]
    factor = 1.0 / math.sqrt(head_size)
    query_heads = queries.astype(jnp.float32).reshape(frame_count, HEADS, head_size)
    key_heads = key_value[:, :inner_width].astype(jnp.float32).reshape(key_span, HEADS, head_size)
    value_heads = key_value[:, inner_width:].astype(jnp.float32).reshape(key_span, HEADS, head_size)
    cot_heads = cotangent.astype(jnp.float32).reshape(frame_count, HEADS, head_size)
    scores = jnp.einsum('fhd,shd->hfs', query_heads, key_heads) * factor
    scores = jnp.where(allowed[None], scores, -jnp.inf)
    maxima = lax.optimization_barrier(jnp.max(scores, axis=-1, keepdims=True))
    shifted = jnp.exp(scores - maxima)
    totals = lax.optimization_barrier(jnp.sum(shifted, axis=-1, keepdims=True))
    weights = shifted / totals
    rounded = weights.astype(jnp.bfloat16)
    rounded_f = rounded.astype(jnp.float32)
    context = jnp.einsum('hfs,shd->fhd', rounded_f, value_heads) * living[:, None, None]
    context = context.reshape(frame_count, inner_width).astype(jnp.bfloat16)
    grad_probs = jnp.einsum('fhd,shd->hfs', cot_heads, value_heads)
    centre_term = lax.optimization_barrier(jnp.sum(grad_probs * weights, axis=-1, keepdims=True))
    grad_scores = (weights * (grad_probs - centre_term) * factor).astype(jnp.bfloat16).astype(jnp.float32)
    grad_query = jnp.einsum('hfs,shd->fhd', grad_scores, key_heads).reshape(frame_count, inner_width)
    grad_key = jnp.einsum('hfs,fhd->shd', grad_scores, query_heads).reshape(key_span, inner_width)
    grad_value = jnp.einsum('hfs,fhd->shd', rounded_f, cot_heads).reshape(key_span, inner_width)
    return (context, grad_query.astype(jnp.bfloat16), jnp.concatenate([grad_key, grad_value], axis=1))

def reference(frames_in, w_qkv, out_grad, lengths):
    call_count, frame_total, model_width = frames_in.shape
    inner_width = w_qkv.shape[1] // 3
    block_count = frame_total // FRAMES_DEV

    def one_call(carry, items):
        frame_rows, cot_rows, length_now = items
        qkv = jnp.dot(frame_rows, w_qkv, preferred_element_type=jnp.float32).astype(jnp.bfloat16)
        queries = qkv[:, :inner_width]
        padded = jnp.pad(qkv[:, inner_width:], ((WIN, WIN), (0, 0)))
        frame_pos = jnp.arange(frame_total, dtype=jnp.int32)
        cotangent_all = jnp.where((frame_pos < length_now)[:, None], cot_rows, jnp.zeros_like(cot_rows))

        def one_block(block_index):
            offset = (block_index * FRAMES_DEV).astype(jnp.int32)
            block_q = lax.dynamic_slice_in_dim(queries, offset, FRAMES_DEV, 0)
            block_kv = lax.dynamic_slice_in_dim(padded, offset, FRAMES_DEV + 2 * WIN, 0)
            block_cot = lax.dynamic_slice_in_dim(cotangent_all, offset, FRAMES_DEV, 0)
            query_pos = offset + jnp.arange(FRAMES_DEV, dtype=jnp.int32)
            key_pos = offset - WIN + jnp.arange(FRAMES_DEV + 2 * WIN, dtype=jnp.int32)
            allowed = band_mask(query_pos, key_pos, length_now)
            living = (query_pos < length_now).astype(jnp.float32)
            return attend(block_q, block_kv, block_cot, allowed, living)
        context, grad_query, grad_terms = lax.map(one_block, jnp.arange(block_count, dtype=jnp.int32))
        own_part = grad_terms[:, WIN:WIN + FRAMES_DEV]
        left_part = lax.optimization_barrier(grad_terms[:, :WIN].astype(jnp.bfloat16)).astype(jnp.float32)
        right_part = lax.optimization_barrier(grad_terms[:, WIN + FRAMES_DEV:].astype(jnp.bfloat16)).astype(jnp.float32)
        blank = jnp.zeros((1, WIN, 2 * inner_width), jnp.float32)
        from_left = jnp.concatenate([blank, right_part[:-1]], axis=0)
        from_right = jnp.concatenate([left_part[1:], blank], axis=0)
        summed = own_part + jnp.pad(from_left, ((0, 0), (0, FRAMES_DEV - WIN), (0, 0)))
        summed = summed + jnp.pad(from_right, ((0, 0), (FRAMES_DEV - WIN, 0), (0, 0)))
        grad_kv = summed.astype(jnp.bfloat16).reshape(frame_total, 2 * inner_width)
        grad_all = jnp.concatenate([grad_query.reshape(frame_total, inner_width), grad_kv], axis=1)
        in_grad = jnp.dot(grad_all, w_qkv.T, preferred_element_type=jnp.float32).astype(jnp.bfloat16)
        term = jnp.dot(frame_rows.T, grad_all, preferred_element_type=jnp.float32)
        return (carry + term, (context.reshape(frame_total, inner_width), in_grad))
    start_grad = jnp.zeros((model_width, 3 * inner_width), jnp.float32)
    weight_grad, outputs = lax.scan(one_call, start_grad, (frames_in, out_grad, lengths))
    return (outputs[0], outputs[1], weight_grad)
```

```python
import math

import jax
import jax.numpy as jnp
from jax import lax
from jax.sharding import PartitionSpec as P

HEADS = 4
WIN = 128


def with_halo(cells, sides, width):
    for axis, dim in sides:
        count = lax.axis_size(axis)
        ends = count - 1
        head = lax.slice_in_dim(cells, 0, width, axis=dim)
        tail = lax.slice_in_dim(cells, cells.shape[dim] - width, cells.shape[dim], axis=dim)
        cells = jnp.concatenate(
            [
                lax.ppermute(tail, axis, [(i, (i + 1) % count) for i in range(ends)]),
                cells,
                lax.ppermute(head, axis, [((i + 1) % count, i) for i in range(ends)]),
            ],
            axis=dim,
        )
    return cells


def band_mask(query_pos, key_pos, length_now):
    gap = jnp.abs(query_pos[:, None] - key_pos[None, :])
    inside = (gap <= WIN) & (key_pos[None, :] >= 0) & (key_pos[None, :] < length_now)
    return inside | (query_pos[:, None] == key_pos[None, :])


def attend(queries, key_value, cotangent, allowed, living):
    frame_count, inner_width = queries.shape
    head_size = inner_width // HEADS
    key_span = key_value.shape[0]
    factor = 1.0 / math.sqrt(head_size)
    query_heads = queries.reshape(frame_count, HEADS, head_size)
    key_heads = key_value[:, :inner_width].reshape(key_span, HEADS, head_size)
    value_heads = key_value[:, inner_width:].reshape(key_span, HEADS, head_size)
    cot_heads = cotangent.reshape(frame_count, HEADS, head_size)
    scores = (
        jnp.einsum("fhd,shd->hfs", query_heads, key_heads, preferred_element_type=jnp.float32)
        * factor
    )
    scores = jnp.where(allowed[None], scores, -jnp.inf)
    maxima = jnp.max(scores, axis=-1, keepdims=True)
    shifted = jnp.exp(scores - maxima)
    totals = jnp.sum(shifted, axis=-1, keepdims=True)
    weights = shifted / totals
    rounded = weights.astype(jnp.bfloat16)
    context = jnp.einsum("hfs,shd->fhd", rounded, value_heads, preferred_element_type=jnp.float32)
    context = (
        (context * living[:, None, None]).reshape(frame_count, inner_width).astype(jnp.bfloat16)
    )
    grad_probs = jnp.einsum(
        "fhd,shd->hfs", cot_heads, value_heads, preferred_element_type=jnp.float32
    )
    centre_term = jnp.sum(grad_probs * weights, axis=-1, keepdims=True)
    grad_scores = (weights * (grad_probs - centre_term) * factor).astype(jnp.bfloat16)
    grad_query = jnp.einsum(
        "hfs,shd->fhd", grad_scores, key_heads, preferred_element_type=jnp.float32
    )
    grad_key = jnp.einsum(
        "hfs,fhd->shd", grad_scores, query_heads, preferred_element_type=jnp.float32
    )
    grad_value = jnp.einsum("hfs,fhd->shd", rounded, cot_heads, preferred_element_type=jnp.float32)
    grad_query = grad_query.reshape(frame_count, inner_width).astype(jnp.bfloat16)
    grad_terms = jnp.concatenate(
        [grad_key.reshape(key_span, inner_width), grad_value.reshape(key_span, inner_width)], axis=1
    )
    return (context, grad_query, grad_terms)


def body(frames_in, w_qkv, out_grad, lengths):
    frame_rows = frames_in[0]
    frame_count, model_width = frame_rows.shape
    inner_width = w_qkv.shape[1] // 3
    window = WIN
    offset = lax.axis_index("ctx") * frame_count
    length_now = lengths[0]
    qkv = jnp.dot(frame_rows, w_qkv, preferred_element_type=jnp.float32).astype(jnp.bfloat16)
    queries = qkv[:, :inner_width]
    key_value = with_halo(qkv[:, inner_width:], (("ctx", 0),), window)
    query_pos = offset + jnp.arange(frame_count, dtype=jnp.int32)
    key_pos = offset - window + jnp.arange(frame_count + 2 * window, dtype=jnp.int32)
    allowed = band_mask(query_pos, key_pos, length_now)
    live_rows = query_pos < length_now
    living = live_rows.astype(jnp.float32)
    cotangent = jnp.where(live_rows[:, None], out_grad[0], jnp.zeros_like(out_grad[0]))
    context, grad_query, grad_terms = attend(queries, key_value, cotangent, allowed, living)
    own_part = grad_terms[window : window + frame_count]
    rim_part = jnp.concatenate(
        [grad_terms[:window], grad_terms[window + frame_count :]], axis=0
    ).astype(jnp.bfloat16)
    returned = with_halo(rim_part, (("ctx", 0),), window)
    from_left = returned[:window].astype(jnp.float32)
    from_right = returned[3 * window :].astype(jnp.float32)
    summed = own_part + from_left
    summed = summed + from_right
    grad_kv = summed.astype(jnp.bfloat16)
    grad_all = jnp.concatenate([grad_query, grad_kv], axis=1)
    in_grad = lax.dot_general(
        grad_all, w_qkv, (((1,), (1,)), ((), ())), preferred_element_type=jnp.float32
    ).astype(jnp.bfloat16)
    row_blocks = lax.axis_size("calls")
    col_blocks = lax.axis_size("ctx")
    row_width = model_width // row_blocks
    col_width = grad_all.shape[1] // col_blocks
    term = jnp.einsum(
        "fas,fbt->abst",
        frame_rows.reshape(frame_count, row_blocks, row_width),
        grad_all.reshape(frame_count, col_blocks, col_width),
        preferred_element_type=jnp.float32,
    ).reshape(row_blocks * col_blocks, row_width * col_width)
    weight_grad = lax.psum_scatter(term, ("calls", "ctx"), scatter_dimension=0, tiled=True)
    weight_grad = weight_grad.reshape(row_width, col_width)
    return (context[None], in_grad[None], weight_grad)


def solution(mesh):
    in_specs = (P("calls", "ctx", None), P(), P("calls", "ctx", None), P("calls"))
    out_specs = (P("calls", "ctx", None), P("calls", "ctx", None), P("calls", "ctx"))
    return jax.shard_map(body, mesh=mesh, in_specs=in_specs, out_specs=out_specs, check_vma=False)
```

```python
import math

import jax
import jax.numpy as jnp
from jax import lax
from jax.sharding import PartitionSpec as P

HEADS = 4
WIN = 128


def with_halo(cells, sides, width):
    for axis, dim in sides:
        count = lax.axis_size(axis)
        ends = count - 1
        head = lax.slice_in_dim(cells, 0, width, axis=dim)
        tail = lax.slice_in_dim(cells, cells.shape[dim] - width, cells.shape[dim], axis=dim)
        cells = jnp.concatenate(
            [
                lax.ppermute(tail, axis, [(i, (i + 1) % count) for i in range(ends)]),
                cells,
                lax.ppermute(head, axis, [((i + 1) % count, i) for i in range(ends)]),
            ],
            axis=dim,
        )
    return cells


def band_mask(query_pos, key_pos, length_now):
    gap = jnp.abs(query_pos[:, None] - key_pos[None, :])
    inside = (gap <= WIN) & (key_pos[None, :] >= 0) & (key_pos[None, :] < length_now)
    return inside | (query_pos[:, None] == key_pos[None, :])


def attend(queries, key_value, cotangent, allowed, living):
    frame_count, inner_width = queries.shape
    head_size = inner_width // HEADS
    key_span = key_value.shape[0]
    factor = 1.0 / math.sqrt(head_size)
    query_heads = queries.reshape(frame_count, HEADS, head_size)
    key_heads = key_value[:, :inner_width].reshape(key_span, HEADS, head_size)
    value_heads = key_value[:, inner_width:].reshape(key_span, HEADS, head_size)
    cot_heads = cotangent.reshape(frame_count, HEADS, head_size)
    scores = (
        jnp.einsum("fhd,shd->hfs", query_heads, key_heads, preferred_element_type=jnp.float32)
        * factor
    )
    scores = jnp.where(allowed[None], scores, -jnp.inf)
    maxima = jnp.max(scores, axis=-1, keepdims=True)
    shifted = jnp.exp(scores - maxima)
    totals = jnp.sum(shifted, axis=-1, keepdims=True)
    weights = shifted / totals
    rounded = weights.astype(jnp.bfloat16)
    context = jnp.einsum("hfs,shd->fhd", rounded, value_heads, preferred_element_type=jnp.float32)
    context = (
        (context * living[:, None, None]).reshape(frame_count, inner_width).astype(jnp.bfloat16)
    )
    grad_probs = jnp.einsum(
        "fhd,shd->hfs", cot_heads, value_heads, preferred_element_type=jnp.float32
    )
    centre_term = jnp.sum(grad_probs * weights, axis=-1, keepdims=True)
    grad_scores = (weights * (grad_probs - centre_term) * factor).astype(jnp.bfloat16)
    grad_query = jnp.einsum(
        "hfs,shd->fhd", grad_scores, key_heads, preferred_element_type=jnp.float32
    )
    grad_key = jnp.einsum(
        "hfs,fhd->shd", grad_scores, query_heads, preferred_element_type=jnp.float32
    )
    grad_value = jnp.einsum("hfs,fhd->shd", rounded, cot_heads, preferred_element_type=jnp.float32)
    grad_query = grad_query.reshape(frame_count, inner_width).astype(jnp.bfloat16)
    grad_terms = jnp.concatenate(
        [grad_key.reshape(key_span, inner_width), grad_value.reshape(key_span, inner_width)], axis=1
    )
    return (context, grad_query, grad_terms)


def weight_gradient(frame_rows, grad_all):
    frame_count, model_width = frame_rows.shape
    grad_width = grad_all.shape[1]
    calls = lax.axis_size("calls")
    ctx = lax.axis_size("ctx")
    row_parts = 4
    col_parts = ctx // row_parts
    tile_rows = model_width // row_parts
    tile_cols = grad_width // col_parts
    block_rows = model_width // calls
    block_cols = grad_width // ctx
    rows_per_tile = tile_rows // block_rows
    cols_per_tile = tile_cols // block_cols
    row_factor = frame_rows.reshape(frame_count, row_parts, 1, tile_rows).transpose(1, 2, 0, 3)
    col_factor = grad_all.reshape(frame_count, 1, col_parts, tile_cols).transpose(1, 2, 0, 3)
    row_factor = jnp.broadcast_to(row_factor, (row_parts, col_parts, frame_count, tile_rows))
    col_factor = jnp.broadcast_to(col_factor, (row_parts, col_parts, frame_count, tile_cols))
    sent = jnp.concatenate([row_factor, col_factor], axis=3).reshape(ctx, frame_count, -1)
    got = lax.all_to_all(sent, "ctx", 0, 0, tiled=True)
    tile = jnp.einsum(
        "sfa,sfb->ab", got[..., :tile_rows], got[..., tile_rows:], preferred_element_type=jnp.float32
    )
    pieces = tile.reshape(rows_per_tile, block_rows, cols_per_tile, block_cols).transpose(0, 2, 1, 3)
    pieces = pieces.reshape(calls, block_rows, block_cols)
    summed = jnp.sum(lax.all_to_all(pieces, "calls", 0, 0, tiled=True), axis=0)
    pairs = []
    for piece in range(calls):
        for owner in range(ctx):
            row_block = (owner // col_parts) * rows_per_tile + piece // cols_per_tile
            col_block = (owner % col_parts) * cols_per_tile + piece % cols_per_tile
            pairs.append((piece * ctx + owner, row_block * ctx + col_block))
    return lax.ppermute(summed, ("calls", "ctx"), pairs)


def body(frames_in, w_qkv, out_grad, lengths):
    frame_rows = frames_in[0]
    frame_count, model_width = frame_rows.shape
    inner_width = w_qkv.shape[1] // 3
    window = WIN
    offset = lax.axis_index("ctx") * frame_count
    length_now = lengths[0]
    qkv = jnp.dot(frame_rows, w_qkv, preferred_element_type=jnp.float32).astype(jnp.bfloat16)
    queries = qkv[:, :inner_width]
    key_value = with_halo(qkv[:, inner_width:], (("ctx", 0),), window)
    query_pos = offset + jnp.arange(frame_count, dtype=jnp.int32)
    key_pos = offset - window + jnp.arange(frame_count + 2 * window, dtype=jnp.int32)
    allowed = band_mask(query_pos, key_pos, length_now)
    live_rows = query_pos < length_now
    living = live_rows.astype(jnp.float32)
    cotangent = jnp.where(live_rows[:, None], out_grad[0], jnp.zeros_like(out_grad[0]))
    context, grad_query, grad_terms = attend(queries, key_value, cotangent, allowed, living)
    own_part = grad_terms[window : window + frame_count]
    rim_part = jnp.concatenate(
        [grad_terms[:window], grad_terms[window + frame_count :]], axis=0
    ).astype(jnp.bfloat16)
    returned = with_halo(rim_part, (("ctx", 0),), window)
    from_left = returned[:window].astype(jnp.float32)
    from_right = returned[3 * window :].astype(jnp.float32)
    summed = own_part + from_left
    summed = summed + from_right
    grad_kv = summed.astype(jnp.bfloat16)
    grad_all = jnp.concatenate([grad_query, grad_kv], axis=1)
    in_grad = lax.dot_general(
        grad_all, w_qkv, (((1,), (1,)), ((), ())), preferred_element_type=jnp.float32
    ).astype(jnp.bfloat16)
    weight_grad = weight_gradient(frame_rows, grad_all)
    return (context[None], in_grad[None], weight_grad)


def solution(mesh):
    in_specs = (P("calls", "ctx", None), P(), P("calls", "ctx", None), P("calls"))
    out_specs = (P("calls", "ctx", None), P("calls", "ctx", None), P("calls", "ctx"))
    return jax.shard_map(body, mesh=mesh, in_specs=in_specs, out_specs=out_specs, check_vma=False)
```

```python
import math

import jax
import jax.numpy as jnp
from jax import lax
from jax.sharding import PartitionSpec as P

HEADS = 4
WIN = 128


def with_halo(cells, sides, width):
    for axis, dim in sides:
        count = lax.axis_size(axis)
        ends = count - 1
        head = lax.slice_in_dim(cells, 0, width, axis=dim)
        tail = lax.slice_in_dim(cells, cells.shape[dim] - width, cells.shape[dim], axis=dim)
        cells = jnp.concatenate(
            [
                lax.ppermute(tail, axis, [(i, (i + 1) % count) for i in range(ends)]),
                cells,
                lax.ppermute(head, axis, [((i + 1) % count, i) for i in range(ends)]),
            ],
            axis=dim,
        )
    return cells


def band_mask(query_pos, key_pos, length_now):
    gap = jnp.abs(query_pos[:, None] - key_pos[None, :])
    inside = (gap <= WIN) & (key_pos[None, :] >= 0) & (key_pos[None, :] < length_now)
    return inside | (query_pos[:, None] == key_pos[None, :])


def attend(queries, key_value, cotangent, allowed, living):
    frame_count, inner_width = queries.shape
    head_size = inner_width // HEADS
    key_span = key_value.shape[0]
    factor = 1.0 / math.sqrt(head_size)
    query_heads = queries.reshape(frame_count, HEADS, head_size)
    key_heads = key_value[:, :inner_width].reshape(key_span, HEADS, head_size)
    value_heads = key_value[:, inner_width:].reshape(key_span, HEADS, head_size)
    cot_heads = cotangent.reshape(frame_count, HEADS, head_size)
    scores = (
        jnp.einsum("fhd,shd->hfs", query_heads, key_heads, preferred_element_type=jnp.float32)
        * factor
    )
    scores = jnp.where(allowed[None], scores, -jnp.inf)
    maxima = jnp.max(scores, axis=-1, keepdims=True)
    shifted = jnp.exp(scores - maxima)
    totals = jnp.sum(shifted, axis=-1, keepdims=True)
    weights = shifted / totals
    rounded = weights.astype(jnp.bfloat16)
    context = jnp.einsum("hfs,shd->fhd", rounded, value_heads, preferred_element_type=jnp.float32)
    context = (
        (context * living[:, None, None]).reshape(frame_count, inner_width).astype(jnp.bfloat16)
    )
    grad_probs = jnp.einsum(
        "fhd,shd->hfs", cot_heads, value_heads, preferred_element_type=jnp.float32
    )
    centre_term = jnp.sum(grad_probs * weights, axis=-1, keepdims=True)
    grad_scores = (weights * (grad_probs - centre_term) * factor).astype(jnp.bfloat16)
    grad_query = jnp.einsum(
        "hfs,shd->fhd", grad_scores, key_heads, preferred_element_type=jnp.float32
    )
    grad_key = jnp.einsum(
        "hfs,fhd->shd", grad_scores, query_heads, preferred_element_type=jnp.float32
    )
    grad_value = jnp.einsum("hfs,fhd->shd", rounded, cot_heads, preferred_element_type=jnp.float32)
    grad_query = grad_query.reshape(frame_count, inner_width).astype(jnp.bfloat16)
    grad_terms = jnp.concatenate(
        [grad_key.reshape(key_span, inner_width), grad_value.reshape(key_span, inner_width)], axis=1
    )
    return (context, grad_query, grad_terms)


def weight_gradient(frame_rows, grad_all):
    frame_count, model_width = frame_rows.shape
    grad_width = grad_all.shape[1]
    calls = lax.axis_size("calls")
    ctx = lax.axis_size("ctx")
    row_parts = 4
    col_parts = ctx // row_parts
    tile_rows = model_width // row_parts
    tile_cols = grad_width // col_parts
    block_rows = model_width // calls
    block_cols = grad_width // ctx
    rows_per_tile = tile_rows // block_rows
    cols_per_tile = tile_cols // block_cols
    row_factor = frame_rows.reshape(frame_count, row_parts, 1, tile_rows).transpose(1, 2, 0, 3)
    col_factor = grad_all.reshape(frame_count, 1, col_parts, tile_cols).transpose(1, 2, 0, 3)
    row_factor = jnp.broadcast_to(row_factor, (row_parts, col_parts, frame_count, tile_rows))
    col_factor = jnp.broadcast_to(col_factor, (row_parts, col_parts, frame_count, tile_cols))
    got_rows = lax.all_to_all(row_factor.reshape(ctx, 2 * frame_count, -1), "ctx", 0, 0, tiled=True)
    got_cols = lax.all_to_all(col_factor.reshape(ctx, frame_count, -1), "ctx", 0, 0, tiled=True)
    got_rows = got_rows.reshape(ctx, frame_count, tile_rows)
    tile = jnp.einsum("sfa,sfb->ab", got_rows, got_cols, preferred_element_type=jnp.float32)
    pieces = tile.reshape(rows_per_tile, block_rows, cols_per_tile, block_cols).transpose(0, 2, 1, 3)
    pieces = pieces.reshape(calls, block_rows, block_cols)
    summed = jnp.sum(lax.all_to_all(pieces, "calls", 0, 0, tiled=True), axis=0)
    pairs = []
    for piece in range(calls):
        for owner in range(ctx):
            row_block = (owner // col_parts) * rows_per_tile + piece // cols_per_tile
            col_block = (owner % col_parts) * cols_per_tile + piece % cols_per_tile
            pairs.append((piece * ctx + owner, row_block * ctx + col_block))
    return lax.ppermute(summed, ("calls", "ctx"), pairs)


def body(frames_in, w_qkv, out_grad, lengths):
    frame_rows = frames_in[0]
    frame_count, model_width = frame_rows.shape
    inner_width = w_qkv.shape[1] // 3
    window = WIN
    offset = lax.axis_index("ctx") * frame_count
    length_now = lengths[0]
    qkv = jnp.dot(frame_rows, w_qkv, preferred_element_type=jnp.float32).astype(jnp.bfloat16)
    queries = qkv[:, :inner_width]
    key_value = with_halo(qkv[:, inner_width:], (("ctx", 0),), window)
    query_pos = offset + jnp.arange(frame_count, dtype=jnp.int32)
    key_pos = offset - window + jnp.arange(frame_count + 2 * window, dtype=jnp.int32)
    allowed = band_mask(query_pos, key_pos, length_now)
    live_rows = query_pos < length_now
    living = live_rows.astype(jnp.float32)
    cotangent = jnp.where(live_rows[:, None], out_grad[0], jnp.zeros_like(out_grad[0]))
    context, grad_query, grad_terms = attend(queries, key_value, cotangent, allowed, living)
    own_part = grad_terms[window : window + frame_count]
    rim_part = jnp.concatenate(
        [grad_terms[:window], grad_terms[window + frame_count :]], axis=0
    ).astype(jnp.bfloat16)
    returned = with_halo(rim_part, (("ctx", 0),), window)
    from_left = returned[:window].astype(jnp.float32)
    from_right = returned[3 * window :].astype(jnp.float32)
    summed = own_part + from_left
    summed = summed + from_right
    grad_kv = summed.astype(jnp.bfloat16)
    grad_all = jnp.concatenate([grad_query, grad_kv], axis=1)
    in_grad = lax.dot_general(
        grad_all, w_qkv, (((1,), (1,)), ((), ())), preferred_element_type=jnp.float32
    ).astype(jnp.bfloat16)
    weight_grad = weight_gradient(frame_rows, grad_all)
    return (context[None], in_grad[None], weight_grad)


def solution(mesh):
    in_specs = (P("calls", "ctx", None), P(), P("calls", "ctx", None), P("calls"))
    out_specs = (P("calls", "ctx", None), P("calls", "ctx", None), P("calls", "ctx"))
    return jax.shard_map(body, mesh=mesh, in_specs=in_specs, out_specs=out_specs, check_vma=False)
```

```python
import math

import jax
import jax.numpy as jnp
from jax import lax
from jax.sharding import PartitionSpec as P

HEADS = 4
WIN = 128


def with_halo(cells, sides, width):
    for axis, dim in sides:
        count = lax.axis_size(axis)
        ends = count - 1
        head = lax.slice_in_dim(cells, 0, width, axis=dim)
        tail = lax.slice_in_dim(cells, cells.shape[dim] - width, cells.shape[dim], axis=dim)
        cells = jnp.concatenate(
            [
                lax.ppermute(tail, axis, [(i, (i + 1) % count) for i in range(ends)]),
                cells,
                lax.ppermute(head, axis, [((i + 1) % count, i) for i in range(ends)]),
            ],
            axis=dim,
        )
    return cells


def band_mask(query_pos, key_pos, length_now):
    gap = jnp.abs(query_pos[:, None] - key_pos[None, :])
    inside = (gap <= WIN) & (key_pos[None, :] >= 0) & (key_pos[None, :] < length_now)
    return inside | (query_pos[:, None] == key_pos[None, :])


def attend(queries, key_value, cotangent, allowed, living):
    frame_count, inner_width = queries.shape
    head_size = inner_width // HEADS
    key_span = key_value.shape[0]
    factor = 1.0 / math.sqrt(head_size)
    query_heads = queries.reshape(frame_count, HEADS, head_size)
    key_heads = key_value[:, :inner_width].reshape(key_span, HEADS, head_size)
    value_heads = key_value[:, inner_width:].reshape(key_span, HEADS, head_size)
    cot_heads = cotangent.reshape(frame_count, HEADS, head_size)
    scores = (
        jnp.einsum("fhd,shd->hfs", query_heads, key_heads, preferred_element_type=jnp.float32)
        * factor
    )
    scores = jnp.where(allowed[None], scores, -jnp.inf)
    maxima = jnp.max(scores, axis=-1, keepdims=True)
    shifted = jnp.exp(scores - maxima)
    totals = jnp.sum(shifted, axis=-1, keepdims=True)
    weights = shifted / totals
    rounded = weights.astype(jnp.bfloat16)
    context = jnp.einsum("hfs,shd->fhd", rounded, value_heads, preferred_element_type=jnp.float32)
    context = (
        (context * living[:, None, None]).reshape(frame_count, inner_width).astype(jnp.bfloat16)
    )
    grad_probs = jnp.einsum(
        "fhd,shd->hfs", cot_heads, value_heads, preferred_element_type=jnp.float32
    )
    centre_term = jnp.sum(grad_probs * weights, axis=-1, keepdims=True)
    grad_scores = (weights * (grad_probs - centre_term) * factor).astype(jnp.bfloat16)
    grad_query = jnp.einsum(
        "hfs,shd->fhd", grad_scores, key_heads, preferred_element_type=jnp.float32
    )
    grad_key = jnp.einsum(
        "hfs,fhd->shd", grad_scores, query_heads, preferred_element_type=jnp.float32
    )
    grad_value = jnp.einsum("hfs,fhd->shd", rounded, cot_heads, preferred_element_type=jnp.float32)
    grad_query = grad_query.reshape(frame_count, inner_width).astype(jnp.bfloat16)
    grad_terms = jnp.concatenate(
        [grad_key.reshape(key_span, inner_width), grad_value.reshape(key_span, inner_width)], axis=1
    )
    return (context, grad_query, grad_terms)


def weight_gradient(frame_rows, grad_all):
    frame_count, model_width = frame_rows.shape
    grad_width = grad_all.shape[1]
    calls = lax.axis_size("calls")
    ctx = lax.axis_size("ctx")
    row_parts = 4
    col_parts = ctx // row_parts
    tile_rows = model_width // row_parts
    tile_cols = grad_width // col_parts
    block_rows = model_width // calls
    block_cols = grad_width // ctx
    rows_per_tile = tile_rows // block_rows
    cols_per_tile = tile_cols // block_cols
    row_factor = frame_rows.reshape(frame_count, row_parts, 1, tile_rows).transpose(1, 2, 0, 3)
    col_factor = grad_all.reshape(frame_count, 1, col_parts, tile_cols).transpose(1, 2, 0, 3)
    row_factor = jnp.broadcast_to(row_factor, (row_parts, col_parts, frame_count, tile_rows))
    col_factor = jnp.broadcast_to(col_factor, (row_parts, col_parts, frame_count, tile_cols))
    sent = jnp.concatenate([row_factor, col_factor], axis=3).reshape(ctx, frame_count, -1)
    got = lax.all_to_all(sent, "ctx", 0, 0, tiled=True)
    row_pieces = got[..., :tile_rows].reshape(ctx, frame_count, rows_per_tile, block_rows)
    col_pieces = got[..., tile_rows:].reshape(ctx, frame_count, cols_per_tile, block_cols)
    pieces = jnp.einsum("sfia,sfjb->ijab", row_pieces, col_pieces, preferred_element_type=jnp.float32)
    pieces = pieces.reshape((2,) * (calls.bit_length() - 1) + (block_rows, block_cols))
    index = lax.axis_index("calls")
    for bit in range(calls.bit_length() - 1):
        axis = pieces.ndim - 3
        mine = (index >> bit) & 1
        low = lax.index_in_dim(pieces, 0, axis, keepdims=False)
        high = lax.index_in_dim(pieces, 1, axis, keepdims=False)
        keep = jnp.where(mine == 0, low, high)
        send = jnp.where(mine == 0, high, low)
        pairs = [(i, i ^ (1 << bit)) for i in range(calls)]
        pieces = keep + lax.ppermute(send, "calls", pairs)
    summed = pieces
    pairs = []
    for piece in range(calls):
        for owner in range(ctx):
            row_block = (owner // col_parts) * rows_per_tile + piece // cols_per_tile
            col_block = (owner % col_parts) * cols_per_tile + piece % cols_per_tile
            pairs.append((piece * ctx + owner, row_block * ctx + col_block))
    return lax.ppermute(summed, ("calls", "ctx"), pairs)


def body(frames_in, w_qkv, out_grad, lengths):
    frame_rows = frames_in[0]
    frame_count, model_width = frame_rows.shape
    inner_width = w_qkv.shape[1] // 3
    window = WIN
    offset = lax.axis_index("ctx") * frame_count
    length_now = lengths[0]
    qkv = jnp.dot(frame_rows, w_qkv, preferred_element_type=jnp.float32).astype(jnp.bfloat16)
    queries = qkv[:, :inner_width]
    key_value = with_halo(qkv[:, inner_width:], (("ctx", 0),), window)
    query_pos = offset + jnp.arange(frame_count, dtype=jnp.int32)
    key_pos = offset - window + jnp.arange(frame_count + 2 * window, dtype=jnp.int32)
    allowed = band_mask(query_pos, key_pos, length_now)
    live_rows = query_pos < length_now
    living = live_rows.astype(jnp.float32)
    cotangent = jnp.where(live_rows[:, None], out_grad[0], jnp.zeros_like(out_grad[0]))
    context, grad_query, grad_terms = attend(queries, key_value, cotangent, allowed, living)
    own_part = grad_terms[window : window + frame_count]
    rim_part = jnp.concatenate(
        [grad_terms[:window], grad_terms[window + frame_count :]], axis=0
    ).astype(jnp.bfloat16)
    returned = with_halo(rim_part, (("ctx", 0),), window)
    from_left = returned[:window].astype(jnp.float32)
    from_right = returned[3 * window :].astype(jnp.float32)
    summed = own_part + from_left
    summed = summed + from_right
    grad_kv = summed.astype(jnp.bfloat16)
    grad_all = jnp.concatenate([grad_query, grad_kv], axis=1)
    in_grad = lax.dot_general(
        grad_all, w_qkv, (((1,), (1,)), ((), ())), preferred_element_type=jnp.float32
    ).astype(jnp.bfloat16)
    weight_grad = weight_gradient(frame_rows, grad_all)
    return (context[None], in_grad[None], weight_grad)


def solution(mesh):
    in_specs = (P("calls", "ctx", None), P(), P("calls", "ctx", None), P("calls"))
    out_specs = (P("calls", "ctx", None), P("calls", "ctx", None), P("calls", "ctx"))
    return jax.shard_map(body, mesh=mesh, in_specs=in_specs, out_specs=out_specs, check_vma=False)
```

```python
import math

import jax
import jax.numpy as jnp
from jax import lax
from jax.sharding import PartitionSpec as P

HEADS = 4
WIN = 128


def with_halo(cells, sides, width):
    for axis, dim in sides:
        count = lax.axis_size(axis)
        ends = count - 1
        head = lax.slice_in_dim(cells, 0, width, axis=dim)
        tail = lax.slice_in_dim(cells, cells.shape[dim] - width, cells.shape[dim], axis=dim)
        cells = jnp.concatenate(
            [
                lax.ppermute(tail, axis, [(i, (i + 1) % count) for i in range(ends)]),
                cells,
                lax.ppermute(head, axis, [((i + 1) % count, i) for i in range(ends)]),
            ],
            axis=dim,
        )
    return cells


def band_mask(query_pos, key_pos, length_now):
    gap = jnp.abs(query_pos[:, None] - key_pos[None, :])
    inside = (gap <= WIN) & (key_pos[None, :] >= 0) & (key_pos[None, :] < length_now)
    return inside | (query_pos[:, None] == key_pos[None, :])


def attend(queries, key_value, cotangent, allowed, living):
    frame_count, inner_width = queries.shape
    head_size = inner_width // HEADS
    key_span = key_value.shape[0]
    factor = 1.0 / math.sqrt(head_size)
    query_heads = queries.reshape(frame_count, HEADS, head_size)
    key_heads = key_value[:, :inner_width].reshape(key_span, HEADS, head_size)
    value_heads = key_value[:, inner_width:].reshape(key_span, HEADS, head_size)
    cot_heads = cotangent.reshape(frame_count, HEADS, head_size)
    scores = (
        jnp.einsum("fhd,shd->hfs", query_heads, key_heads, preferred_element_type=jnp.float32)
        * factor
    )
    scores = jnp.where(allowed[None], scores, -jnp.inf)
    maxima = jnp.max(scores, axis=-1, keepdims=True)
    shifted = jnp.exp(scores - maxima)
    totals = jnp.sum(shifted, axis=-1, keepdims=True)
    weights = shifted / totals
    rounded = weights.astype(jnp.bfloat16)
    context = jnp.einsum("hfs,shd->fhd", rounded, value_heads, preferred_element_type=jnp.float32)
    context = (
        (context * living[:, None, None]).reshape(frame_count, inner_width).astype(jnp.bfloat16)
    )
    grad_probs = jnp.einsum(
        "fhd,shd->hfs", cot_heads, value_heads, preferred_element_type=jnp.float32
    )
    centre_term = jnp.sum(grad_probs * weights, axis=-1, keepdims=True)
    grad_scores = (weights * (grad_probs - centre_term) * factor).astype(jnp.bfloat16)
    grad_query = jnp.einsum(
        "hfs,shd->fhd", grad_scores, key_heads, preferred_element_type=jnp.float32
    )
    grad_key = jnp.einsum(
        "hfs,fhd->shd", grad_scores, query_heads, preferred_element_type=jnp.float32
    )
    grad_value = jnp.einsum("hfs,fhd->shd", rounded, cot_heads, preferred_element_type=jnp.float32)
    grad_query = grad_query.reshape(frame_count, inner_width).astype(jnp.bfloat16)
    grad_terms = jnp.concatenate(
        [grad_key.reshape(key_span, inner_width), grad_value.reshape(key_span, inner_width)], axis=1
    )
    return (context, grad_query, grad_terms)


def weight_gradient(frame_rows, grad_all):
    frame_count, model_width = frame_rows.shape
    grad_width = grad_all.shape[1]
    calls = lax.axis_size("calls")
    ctx = lax.axis_size("ctx")
    row_parts = 4
    col_parts = ctx // row_parts
    tile_rows = model_width // row_parts
    tile_cols = grad_width // col_parts
    block_rows = model_width // calls
    block_cols = grad_width // ctx
    rows_per_tile = tile_rows // block_rows
    cols_per_tile = tile_cols // block_cols
    row_factor = frame_rows.reshape(frame_count, row_parts, 1, tile_rows).transpose(1, 2, 0, 3)
    col_factor = grad_all.reshape(frame_count, 1, col_parts, tile_cols).transpose(1, 2, 0, 3)
    row_factor = jnp.broadcast_to(row_factor, (row_parts, col_parts, frame_count, tile_rows))
    col_factor = jnp.broadcast_to(col_factor, (row_parts, col_parts, frame_count, tile_cols))
    sent = jnp.concatenate([row_factor, col_factor], axis=3).reshape(ctx, frame_count, -1)
    got = lax.all_to_all(sent, "ctx", 0, 0, tiled=True)
    row_pieces = got[..., :tile_rows].reshape(ctx, frame_count, rows_per_tile, 1, block_rows)
    col_pieces = got[..., tile_rows:].reshape(ctx, frame_count, 1, cols_per_tile, block_cols)
    pieces = jnp.einsum(
        "sfiza,sfzjb->ijab", row_pieces, col_pieces, preferred_element_type=jnp.float32
    ).reshape(calls, block_rows, block_cols)
    summed = jnp.sum(lax.all_to_all(pieces, "calls", 0, 0, tiled=True), axis=0)
    pairs = []
    for piece in range(calls):
        for owner in range(ctx):
            row_block = (owner // col_parts) * rows_per_tile + piece // cols_per_tile
            col_block = (owner % col_parts) * cols_per_tile + piece % cols_per_tile
            pairs.append((piece * ctx + owner, row_block * ctx + col_block))
    return lax.ppermute(summed, ("calls", "ctx"), pairs)


def body(frames_in, w_qkv, out_grad, lengths):
    frame_rows = frames_in[0]
    frame_count, model_width = frame_rows.shape
    inner_width = w_qkv.shape[1] // 3
    window = WIN
    offset = lax.axis_index("ctx") * frame_count
    length_now = lengths[0]
    qkv = jnp.dot(frame_rows, w_qkv, preferred_element_type=jnp.float32).astype(jnp.bfloat16)
    queries = qkv[:, :inner_width]
    key_value = with_halo(qkv[:, inner_width:], (("ctx", 0),), window)
    query_pos = offset + jnp.arange(frame_count, dtype=jnp.int32)
    key_pos = offset - window + jnp.arange(frame_count + 2 * window, dtype=jnp.int32)
    allowed = band_mask(query_pos, key_pos, length_now)
    live_rows = query_pos < length_now
    living = live_rows.astype(jnp.float32)
    cotangent = jnp.where(live_rows[:, None], out_grad[0], jnp.zeros_like(out_grad[0]))
    context, grad_query, grad_terms = attend(queries, key_value, cotangent, allowed, living)
    own_part = grad_terms[window : window + frame_count]
    rim_part = jnp.concatenate(
        [grad_terms[:window], grad_terms[window + frame_count :]], axis=0
    ).astype(jnp.bfloat16)
    returned = with_halo(rim_part, (("ctx", 0),), window)
    from_left = returned[:window].astype(jnp.float32)
    from_right = returned[3 * window :].astype(jnp.float32)
    summed = own_part + from_left
    summed = summed + from_right
    grad_kv = summed.astype(jnp.bfloat16)
    grad_all = jnp.concatenate([grad_query, grad_kv], axis=1)
    in_grad = lax.dot_general(
        grad_all, w_qkv, (((1,), (1,)), ((), ())), preferred_element_type=jnp.float32
    ).astype(jnp.bfloat16)
    weight_grad = weight_gradient(frame_rows, grad_all)
    return (context[None], in_grad[None], weight_grad)


def solution(mesh):
    in_specs = (P("calls", "ctx", None), P(), P("calls", "ctx", None), P("calls"))
    out_specs = (P("calls", "ctx", None), P("calls", "ctx", None), P("calls", "ctx"))
    return jax.shard_map(body, mesh=mesh, in_specs=in_specs, out_specs=out_specs, check_vma=False)
```

```python
import math

import jax
import jax.numpy as jnp
from jax import lax
from jax.sharding import Mesh, PartitionSpec as P

HEADS = 4
WIN = 128
CTX = ("cx", "cy")


def with_halo(cells, sides, width):
    for axis, dim in sides:
        count = lax.axis_size(axis)
        ends = count - 1
        head = lax.slice_in_dim(cells, 0, width, axis=dim)
        tail = lax.slice_in_dim(cells, cells.shape[dim] - width, cells.shape[dim], axis=dim)
        cells = jnp.concatenate(
            [
                lax.ppermute(tail, axis, [(i, (i + 1) % count) for i in range(ends)]),
                cells,
                lax.ppermute(head, axis, [((i + 1) % count, i) for i in range(ends)]),
            ],
            axis=dim,
        )
    return cells


def band_mask(query_pos, key_pos, length_now):
    gap = jnp.abs(query_pos[:, None] - key_pos[None, :])
    inside = (gap <= WIN) & (key_pos[None, :] >= 0) & (key_pos[None, :] < length_now)
    return inside | (query_pos[:, None] == key_pos[None, :])


def attend(queries, key_value, cotangent, allowed, living):
    frame_count, inner_width = queries.shape
    head_size = inner_width // HEADS
    key_span = key_value.shape[0]
    factor = 1.0 / math.sqrt(head_size)
    query_heads = queries.reshape(frame_count, HEADS, head_size)
    key_heads = key_value[:, :inner_width].reshape(key_span, HEADS, head_size)
    value_heads = key_value[:, inner_width:].reshape(key_span, HEADS, head_size)
    cot_heads = cotangent.reshape(frame_count, HEADS, head_size)
    scores = (
        jnp.einsum("fhd,shd->hfs", query_heads, key_heads, preferred_element_type=jnp.float32)
        * factor
    )
    scores = jnp.where(allowed[None], scores, -jnp.inf)
    maxima = jnp.max(scores, axis=-1, keepdims=True)
    shifted = jnp.exp(scores - maxima)
    totals = jnp.sum(shifted, axis=-1, keepdims=True)
    weights = shifted / totals
    rounded = weights.astype(jnp.bfloat16)
    context = jnp.einsum("hfs,shd->fhd", rounded, value_heads, preferred_element_type=jnp.float32)
    context = (
        (context * living[:, None, None]).reshape(frame_count, inner_width).astype(jnp.bfloat16)
    )
    grad_probs = jnp.einsum(
        "fhd,shd->hfs", cot_heads, value_heads, preferred_element_type=jnp.float32
    )
    centre_term = jnp.sum(grad_probs * weights, axis=-1, keepdims=True)
    grad_scores = (weights * (grad_probs - centre_term) * factor).astype(jnp.bfloat16)
    grad_query = jnp.einsum(
        "hfs,shd->fhd", grad_scores, key_heads, preferred_element_type=jnp.float32
    )
    grad_key = jnp.einsum(
        "hfs,fhd->shd", grad_scores, query_heads, preferred_element_type=jnp.float32
    )
    grad_value = jnp.einsum("hfs,fhd->shd", rounded, cot_heads, preferred_element_type=jnp.float32)
    grad_query = grad_query.reshape(frame_count, inner_width).astype(jnp.bfloat16)
    grad_terms = jnp.concatenate(
        [grad_key.reshape(key_span, inner_width), grad_value.reshape(key_span, inner_width)], axis=1
    )
    return (context, grad_query, grad_terms)


def weight_gradient(frame_rows, grad_all):
    frame_count, model_width = frame_rows.shape
    grad_width = grad_all.shape[1]
    calls = lax.axis_size("calls")
    ring = lax.axis_size("cx")
    group = lax.axis_size("cy")
    ctx = ring * group
    block_rows = model_width // calls
    block_cols = grad_width // ctx
    tile_rows = model_width // 2
    tile_cols = grad_width // (group // 2)
    row_factor = frame_rows.reshape(frame_count, 2, 1, tile_rows).transpose(1, 2, 0, 3)
    col_factor = grad_all.reshape(frame_count, 1, group // 2, tile_cols).transpose(1, 2, 0, 3)
    row_factor = jnp.broadcast_to(row_factor, (2, group // 2, frame_count, tile_rows))
    col_factor = jnp.broadcast_to(col_factor, (2, group // 2, frame_count, tile_cols))
    sent = jnp.concatenate([row_factor, col_factor], axis=3).reshape(group, frame_count, -1)
    got = lax.all_to_all(sent, "cy", 0, 0, tiled=True)
    pair_rows = tile_rows // (ring * block_rows)
    row_pieces = got[..., :tile_rows].reshape(group, frame_count, ring, pair_rows, 1, block_rows)
    col_pieces = got[..., tile_rows:].reshape(group, frame_count, 1, 1, -1, block_cols)
    parts = jnp.einsum(
        "sfpiza,sfzwjb->pijab", row_pieces, col_pieces, preferred_element_type=jnp.float32
    ).reshape(ring, calls, block_rows * block_cols)
    part = jnp.sum(lax.all_to_all(parts, "cx", 0, 0, tiled=True), axis=0)
    summed = jnp.sum(lax.all_to_all(part, "calls", 0, 0, tiled=True), axis=0)
    summed = summed.reshape(block_rows, block_cols)
    col_pieces_per_tile = tile_cols // block_cols
    pairs = []
    for piece in range(calls):
        for x in range(ring):
            for y in range(group):
                row_block = (y // (group // 2)) * (tile_rows // block_rows)
                row_block += x * pair_rows + piece // col_pieces_per_tile
                col_block = (y % (group // 2)) * col_pieces_per_tile + piece % col_pieces_per_tile
                pairs.append(((piece * ring + x) * group + y, row_block * ctx + col_block))
    return lax.ppermute(summed, ("calls", "cx", "cy"), pairs)


def body(frames_in, w_qkv, out_grad, lengths):
    frame_rows = frames_in[0]
    frame_count, model_width = frame_rows.shape
    inner_width = w_qkv.shape[1] // 3
    window = WIN
    offset = lax.axis_index(CTX) * frame_count
    length_now = lengths[0]
    qkv = jnp.dot(frame_rows, w_qkv, preferred_element_type=jnp.float32).astype(jnp.bfloat16)
    queries = qkv[:, :inner_width]
    key_value = with_halo(qkv[:, inner_width:], ((CTX, 0),), window)
    query_pos = offset + jnp.arange(frame_count, dtype=jnp.int32)
    key_pos = offset - window + jnp.arange(frame_count + 2 * window, dtype=jnp.int32)
    allowed = band_mask(query_pos, key_pos, length_now)
    live_rows = query_pos < length_now
    living = live_rows.astype(jnp.float32)
    cotangent = jnp.where(live_rows[:, None], out_grad[0], jnp.zeros_like(out_grad[0]))
    context, grad_query, grad_terms = attend(queries, key_value, cotangent, allowed, living)
    own_part = grad_terms[window : window + frame_count]
    rim_part = jnp.concatenate(
        [grad_terms[:window], grad_terms[window + frame_count :]], axis=0
    ).astype(jnp.bfloat16)
    returned = with_halo(rim_part, ((CTX, 0),), window)
    from_left = returned[:window].astype(jnp.float32)
    from_right = returned[3 * window :].astype(jnp.float32)
    summed = own_part + from_left
    summed = summed + from_right
    grad_kv = summed.astype(jnp.bfloat16)
    grad_all = jnp.concatenate([grad_query, grad_kv], axis=1)
    in_grad = lax.dot_general(
        grad_all, w_qkv, (((1,), (1,)), ((), ())), preferred_element_type=jnp.float32
    ).astype(jnp.bfloat16)
    weight_grad = weight_gradient(frame_rows, grad_all)
    return (context[None], in_grad[None], weight_grad)


def solution(mesh):
    calls, ctx = mesh.devices.shape
    group = 4
    fine = Mesh(mesh.devices.reshape(calls, ctx // group, group), ("calls",) + CTX)
    frames = P("calls", CTX, None)
    in_specs = (frames, P(), frames, P("calls"))
    out_specs = (frames, frames, P("calls", CTX))
    return jax.shard_map(body, mesh=fine, in_specs=in_specs, out_specs=out_specs, check_vma=False)
```

```python
import math

import jax
import jax.numpy as jnp
from jax import lax
from jax.sharding import Mesh, PartitionSpec as P

HEADS = 4
WIN = 128
CTX = ("cx", "cy")


def with_halo(cells, sides, width):
    for axis, dim in sides:
        count = lax.axis_size(axis)
        ends = count - 1
        head = lax.slice_in_dim(cells, 0, width, axis=dim)
        tail = lax.slice_in_dim(cells, cells.shape[dim] - width, cells.shape[dim], axis=dim)
        cells = jnp.concatenate(
            [
                lax.ppermute(tail, axis, [(i, (i + 1) % count) for i in range(ends)]),
                cells,
                lax.ppermute(head, axis, [((i + 1) % count, i) for i in range(ends)]),
            ],
            axis=dim,
        )
    return cells


def band_mask(query_pos, key_pos, length_now):
    gap = jnp.abs(query_pos[:, None] - key_pos[None, :])
    inside = (gap <= WIN) & (key_pos[None, :] >= 0) & (key_pos[None, :] < length_now)
    return inside | (query_pos[:, None] == key_pos[None, :])


def attend(queries, key_value, cotangent, allowed, living):
    frame_count, inner_width = queries.shape
    head_size = inner_width // HEADS
    key_span = key_value.shape[0]
    factor = 1.0 / math.sqrt(head_size)
    query_heads = queries.reshape(frame_count, HEADS, head_size)
    key_heads = key_value[:, :inner_width].reshape(key_span, HEADS, head_size)
    value_heads = key_value[:, inner_width:].reshape(key_span, HEADS, head_size)
    cot_heads = cotangent.reshape(frame_count, HEADS, head_size)
    scores = (
        jnp.einsum("fhd,shd->hfs", query_heads, key_heads, preferred_element_type=jnp.float32)
        * factor
    )
    scores = jnp.where(allowed[None], scores, -jnp.inf)
    maxima = jnp.max(scores, axis=-1, keepdims=True)
    shifted = jnp.exp(scores - maxima)
    totals = jnp.sum(shifted, axis=-1, keepdims=True)
    weights = shifted / totals
    rounded = weights.astype(jnp.bfloat16)
    context = jnp.einsum("hfs,shd->fhd", rounded, value_heads, preferred_element_type=jnp.float32)
    context = (
        (context * living[:, None, None]).reshape(frame_count, inner_width).astype(jnp.bfloat16)
    )
    grad_probs = jnp.einsum(
        "fhd,shd->hfs", cot_heads, value_heads, preferred_element_type=jnp.float32
    )
    centre_term = jnp.sum(grad_probs * weights, axis=-1, keepdims=True)
    grad_scores = (weights * (grad_probs - centre_term) * factor).astype(jnp.bfloat16)
    grad_query = jnp.einsum(
        "hfs,shd->fhd", grad_scores, key_heads, preferred_element_type=jnp.float32
    )
    grad_key = jnp.einsum(
        "hfs,fhd->shd", grad_scores, query_heads, preferred_element_type=jnp.float32
    )
    grad_value = jnp.einsum("hfs,fhd->shd", rounded, cot_heads, preferred_element_type=jnp.float32)
    grad_query = grad_query.reshape(frame_count, inner_width).astype(jnp.bfloat16)
    grad_terms = jnp.concatenate(
        [grad_key.reshape(key_span, inner_width), grad_value.reshape(key_span, inner_width)], axis=1
    )
    return (context, grad_query, grad_terms)


def weight_gradient(frame_rows, grad_all):
    frame_count, model_width = frame_rows.shape
    grad_width = grad_all.shape[1]
    calls = lax.axis_size("calls")
    ring = lax.axis_size("cx")
    group = lax.axis_size("cy")
    ctx = ring * group
    block_rows = model_width // calls
    block_cols = grad_width // ctx
    tile_rows = model_width // 2
    tile_cols = grad_width // (group // 2)
    row_factor = frame_rows.reshape(frame_count, 2, 1, tile_rows).transpose(1, 2, 0, 3)
    col_factor = grad_all.reshape(frame_count, 1, group // 2, tile_cols).transpose(1, 2, 0, 3)
    row_factor = jnp.broadcast_to(row_factor, (2, group // 2, frame_count, tile_rows))
    col_factor = jnp.broadcast_to(col_factor, (2, group // 2, frame_count, tile_cols))
    sent = jnp.concatenate([row_factor, col_factor], axis=3).reshape(group, frame_count, -1)
    got = lax.all_to_all(sent, "cy", 0, 0, tiled=True)
    pair_rows = tile_rows // (ring * block_rows)
    tile = jnp.einsum(
        "sfa,sfb->ab", got[..., :tile_rows], got[..., tile_rows:], preferred_element_type=jnp.float32
    )
    parts = tile.reshape(ring, pair_rows * block_rows, tile_cols)
    part = jnp.sum(lax.all_to_all(parts, "cx", 0, 0, tiled=True), axis=0)
    part = part.reshape(pair_rows, block_rows, -1, block_cols).transpose(0, 2, 1, 3)
    part = part.reshape(calls, block_rows * block_cols)
    summed = jnp.sum(lax.all_to_all(part, "calls", 0, 0, tiled=True), axis=0)
    summed = summed.reshape(block_rows, block_cols)
    col_pieces_per_tile = tile_cols // block_cols
    pairs = []
    for piece in range(calls):
        for x in range(ring):
            for y in range(group):
                row_block = (y // (group // 2)) * (tile_rows // block_rows)
                row_block += x * pair_rows + piece // col_pieces_per_tile
                col_block = (y % (group // 2)) * col_pieces_per_tile + piece % col_pieces_per_tile
                pairs.append(((piece * ring + x) * group + y, row_block * ctx + col_block))
    return lax.ppermute(summed, ("calls", "cx", "cy"), pairs)


def body(frames_in, w_qkv, out_grad, lengths):
    frame_rows = frames_in[0]
    frame_count, model_width = frame_rows.shape
    inner_width = w_qkv.shape[1] // 3
    window = WIN
    offset = lax.axis_index(CTX) * frame_count
    length_now = lengths[0]
    qkv = jnp.dot(frame_rows, w_qkv, preferred_element_type=jnp.float32).astype(jnp.bfloat16)
    queries = qkv[:, :inner_width]
    key_value = with_halo(qkv[:, inner_width:], ((CTX, 0),), window)
    query_pos = offset + jnp.arange(frame_count, dtype=jnp.int32)
    key_pos = offset - window + jnp.arange(frame_count + 2 * window, dtype=jnp.int32)
    allowed = band_mask(query_pos, key_pos, length_now)
    live_rows = query_pos < length_now
    living = live_rows.astype(jnp.float32)
    cotangent = jnp.where(live_rows[:, None], out_grad[0], jnp.zeros_like(out_grad[0]))
    context, grad_query, grad_terms = attend(queries, key_value, cotangent, allowed, living)
    own_part = grad_terms[window : window + frame_count]
    rim_part = jnp.concatenate(
        [grad_terms[:window], grad_terms[window + frame_count :]], axis=0
    ).astype(jnp.bfloat16)
    returned = with_halo(rim_part, ((CTX, 0),), window)
    from_left = returned[:window].astype(jnp.float32)
    from_right = returned[3 * window :].astype(jnp.float32)
    summed = own_part + from_left
    summed = summed + from_right
    grad_kv = summed.astype(jnp.bfloat16)
    grad_all = jnp.concatenate([grad_query, grad_kv], axis=1)
    in_grad = lax.dot_general(
        grad_all, w_qkv, (((1,), (1,)), ((), ())), preferred_element_type=jnp.float32
    ).astype(jnp.bfloat16)
    weight_grad = weight_gradient(frame_rows, grad_all)
    return (context[None], in_grad[None], weight_grad)


def solution(mesh):
    calls, ctx = mesh.devices.shape
    group = 4
    fine = Mesh(mesh.devices.reshape(calls, ctx // group, group), ("calls",) + CTX)
    frames = P("calls", CTX, None)
    in_specs = (frames, P(), frames, P("calls"))
    out_specs = (frames, frames, P("calls", CTX))
    return jax.shard_map(body, mesh=fine, in_specs=in_specs, out_specs=out_specs, check_vma=False)
```

```python
import math

import jax
import jax.numpy as jnp
from jax import lax
from jax.sharding import Mesh, PartitionSpec as P

HEADS = 4
WIN = 128
CALLS = ("ch", "cz", "cc")
CTX = ("cx", "cy")


def with_halo(cells, sides, width):
    for axis, dim in sides:
        count = lax.axis_size(axis)
        ends = count - 1
        head = lax.slice_in_dim(cells, 0, width, axis=dim)
        tail = lax.slice_in_dim(cells, cells.shape[dim] - width, cells.shape[dim], axis=dim)
        cells = jnp.concatenate(
            [
                lax.ppermute(tail, axis, [(i, (i + 1) % count) for i in range(ends)]),
                cells,
                lax.ppermute(head, axis, [((i + 1) % count, i) for i in range(ends)]),
            ],
            axis=dim,
        )
    return cells


def band_mask(query_pos, key_pos, length_now):
    gap = jnp.abs(query_pos[:, None] - key_pos[None, :])
    inside = (gap <= WIN) & (key_pos[None, :] >= 0) & (key_pos[None, :] < length_now)
    return inside | (query_pos[:, None] == key_pos[None, :])


def attend(queries, key_value, cotangent, allowed, living):
    frame_count, inner_width = queries.shape
    head_size = inner_width // HEADS
    key_span = key_value.shape[0]
    factor = 1.0 / math.sqrt(head_size)
    query_heads = queries.reshape(frame_count, HEADS, head_size)
    key_heads = key_value[:, :inner_width].reshape(key_span, HEADS, head_size)
    value_heads = key_value[:, inner_width:].reshape(key_span, HEADS, head_size)
    cot_heads = cotangent.reshape(frame_count, HEADS, head_size)
    scores = (
        jnp.einsum("fhd,shd->hfs", query_heads, key_heads, preferred_element_type=jnp.float32)
        * factor
    )
    scores = jnp.where(allowed[None], scores, -jnp.inf)
    maxima = jnp.max(scores, axis=-1, keepdims=True)
    shifted = jnp.exp(scores - maxima)
    totals = jnp.sum(shifted, axis=-1, keepdims=True)
    weights = shifted / totals
    rounded = weights.astype(jnp.bfloat16)
    context = jnp.einsum("hfs,shd->fhd", rounded, value_heads, preferred_element_type=jnp.float32)
    context = (
        (context * living[:, None, None]).reshape(frame_count, inner_width).astype(jnp.bfloat16)
    )
    grad_probs = jnp.einsum(
        "fhd,shd->hfs", cot_heads, value_heads, preferred_element_type=jnp.float32
    )
    centre_term = jnp.sum(grad_probs * weights, axis=-1, keepdims=True)
    grad_scores = (weights * (grad_probs - centre_term) * factor).astype(jnp.bfloat16)
    grad_query = jnp.einsum(
        "hfs,shd->fhd", grad_scores, key_heads, preferred_element_type=jnp.float32
    )
    grad_key = jnp.einsum(
        "hfs,fhd->shd", grad_scores, query_heads, preferred_element_type=jnp.float32
    )
    grad_value = jnp.einsum("hfs,fhd->shd", rounded, cot_heads, preferred_element_type=jnp.float32)
    grad_query = grad_query.reshape(frame_count, inner_width).astype(jnp.bfloat16)
    grad_terms = jnp.concatenate(
        [grad_key.reshape(key_span, inner_width), grad_value.reshape(key_span, inner_width)], axis=1
    )
    return (context, grad_query, grad_terms)


def weight_gradient(frame_rows, grad_all):
    frame_count, model_width = frame_rows.shape
    grad_width = grad_all.shape[1]
    calls = lax.axis_size(CALLS)
    pair = lax.axis_size("cc")
    spread = lax.axis_size(CALLS[:2])
    ring = lax.axis_size("cx")
    group = lax.axis_size("cy")
    ctx = ring * group
    block_rows = model_width // calls
    block_cols = grad_width // ctx
    tile_rows = model_width // 2
    tile_cols = grad_width // (group // 2)
    row_factor = frame_rows.reshape(frame_count, 2, 1, tile_rows).transpose(1, 2, 0, 3)
    col_factor = grad_all.reshape(frame_count, 1, group // 2, tile_cols).transpose(1, 2, 0, 3)
    row_factor = jnp.broadcast_to(row_factor, (2, group // 2, frame_count, tile_rows))
    col_factor = jnp.broadcast_to(col_factor, (2, group // 2, frame_count, tile_cols))
    sent = jnp.concatenate([row_factor, col_factor], axis=3).reshape(group, frame_count, -1)
    got = lax.all_to_all(sent, "cy", 0, 0, tiled=True)
    tile = jnp.einsum(
        "sfa,sfb->ab", got[..., :tile_rows], got[..., tile_rows:], preferred_element_type=jnp.float32
    )
    halves = tile.reshape(pair, tile_rows // pair, tile_cols)
    core = lax.axis_index("cc")
    keep = lax.dynamic_index_in_dim(halves, core, 0, keepdims=False)
    send = lax.dynamic_index_in_dim(halves, pair - 1 - core, 0, keepdims=False)
    half = keep + lax.ppermute(send, "cc", [(0, 1), (1, 0)])
    parts = half.reshape(ring, block_rows, tile_cols)
    part = jnp.sum(lax.all_to_all(parts, "cx", 0, 0, tiled=True), axis=0)
    part = part.reshape(block_rows, spread, block_cols).transpose(1, 0, 2)
    part = part.reshape(spread, block_rows * block_cols)
    summed = jnp.sum(lax.all_to_all(part, CALLS[:2], 0, 0, tiled=True), axis=0)
    summed = summed.reshape(block_rows, block_cols)
    pairs = []
    for far in range(spread):
        for near in range(pair):
            for x in range(ring):
                for y in range(group):
                    row_block = ((y // (group // 2)) * pair + near) * ring + x
                    col_block = (y % (group // 2)) * spread + far
                    source = ((far * pair + near) * ring + x) * group + y
                    pairs.append((source, row_block * ctx + col_block))
    return lax.ppermute(summed, CALLS + CTX, pairs)


def body(frames_in, w_qkv, out_grad, lengths):
    frame_rows = frames_in[0]
    frame_count, model_width = frame_rows.shape
    inner_width = w_qkv.shape[1] // 3
    window = WIN
    offset = lax.axis_index(CTX) * frame_count
    length_now = lengths[0]
    qkv = jnp.dot(frame_rows, w_qkv, preferred_element_type=jnp.float32).astype(jnp.bfloat16)
    queries = qkv[:, :inner_width]
    key_value = with_halo(qkv[:, inner_width:], ((CTX, 0),), window)
    query_pos = offset + jnp.arange(frame_count, dtype=jnp.int32)
    key_pos = offset - window + jnp.arange(frame_count + 2 * window, dtype=jnp.int32)
    allowed = band_mask(query_pos, key_pos, length_now)
    live_rows = query_pos < length_now
    living = live_rows.astype(jnp.float32)
    cotangent = jnp.where(live_rows[:, None], out_grad[0], jnp.zeros_like(out_grad[0]))
    context, grad_query, grad_terms = attend(queries, key_value, cotangent, allowed, living)
    own_part = grad_terms[window : window + frame_count]
    rim_part = jnp.concatenate(
        [grad_terms[:window], grad_terms[window + frame_count :]], axis=0
    ).astype(jnp.bfloat16)
    returned = with_halo(rim_part, ((CTX, 0),), window)
    from_left = returned[:window].astype(jnp.float32)
    from_right = returned[3 * window :].astype(jnp.float32)
    summed = own_part + from_left
    summed = summed + from_right
    grad_kv = summed.astype(jnp.bfloat16)
    grad_all = jnp.concatenate([grad_query, grad_kv], axis=1)
    in_grad = lax.dot_general(
        grad_all, w_qkv, (((1,), (1,)), ((), ())), preferred_element_type=jnp.float32
    ).astype(jnp.bfloat16)
    weight_grad = weight_gradient(frame_rows, grad_all)
    return (context[None], in_grad[None], weight_grad)


def solution(mesh):
    calls, ctx = mesh.devices.shape
    pair = 2
    group = 4
    shape = (2, calls // (2 * pair), pair, ctx // group, group)
    fine = Mesh(mesh.devices.reshape(shape), CALLS + CTX)
    frames = P(CALLS, CTX, None)
    in_specs = (frames, P(), frames, P(CALLS))
    out_specs = (frames, frames, P(CALLS, CTX))
    return jax.shard_map(body, mesh=fine, in_specs=in_specs, out_specs=out_specs, check_vma=False)
```

```python
import math

import jax
import jax.numpy as jnp
from jax import lax
from jax.sharding import Mesh, PartitionSpec as P

HEADS = 4
WIN = 128
CALLS = ("ch", "cz", "cc")
CTX = ("cx", "cy")


def with_halo(cells, sides, width):
    for axis, dim in sides:
        count = lax.axis_size(axis)
        ends = count - 1
        head = lax.slice_in_dim(cells, 0, width, axis=dim)
        tail = lax.slice_in_dim(cells, cells.shape[dim] - width, cells.shape[dim], axis=dim)
        cells = jnp.concatenate(
            [
                lax.ppermute(tail, axis, [(i, (i + 1) % count) for i in range(ends)]),
                cells,
                lax.ppermute(head, axis, [((i + 1) % count, i) for i in range(ends)]),
            ],
            axis=dim,
        )
    return cells


def band_mask(query_pos, key_pos, length_now):
    gap = jnp.abs(query_pos[:, None] - key_pos[None, :])
    inside = (gap <= WIN) & (key_pos[None, :] >= 0) & (key_pos[None, :] < length_now)
    return inside | (query_pos[:, None] == key_pos[None, :])


def attend(queries, key_value, cotangent, allowed, living):
    frame_count, inner_width = queries.shape
    head_size = inner_width // HEADS
    key_span = key_value.shape[0]
    factor = 1.0 / math.sqrt(head_size)
    query_heads = queries.reshape(frame_count, HEADS, head_size)
    key_heads = key_value[:, :inner_width].reshape(key_span, HEADS, head_size)
    value_heads = key_value[:, inner_width:].reshape(key_span, HEADS, head_size)
    cot_heads = cotangent.reshape(frame_count, HEADS, head_size)
    scores = (
        jnp.einsum("fhd,shd->hfs", query_heads, key_heads, preferred_element_type=jnp.float32)
        * factor
    )
    scores = jnp.where(allowed[None], scores, -jnp.inf)
    maxima = jnp.max(scores, axis=-1, keepdims=True)
    shifted = jnp.exp(scores - maxima)
    totals = jnp.sum(shifted, axis=-1, keepdims=True)
    weights = shifted / totals
    rounded = weights.astype(jnp.bfloat16)
    context = jnp.einsum("hfs,shd->fhd", rounded, value_heads, preferred_element_type=jnp.float32)
    context = (
        (context * living[:, None, None]).reshape(frame_count, inner_width).astype(jnp.bfloat16)
    )
    grad_probs = jnp.einsum(
        "fhd,shd->hfs", cot_heads, value_heads, preferred_element_type=jnp.float32
    )
    centre_term = jnp.sum(grad_probs * weights, axis=-1, keepdims=True)
    grad_scores = (weights * (grad_probs - centre_term) * factor).astype(jnp.bfloat16)
    grad_query = jnp.einsum(
        "hfs,shd->fhd", grad_scores, key_heads, preferred_element_type=jnp.float32
    )
    grad_key = jnp.einsum(
        "hfs,fhd->shd", grad_scores, query_heads, preferred_element_type=jnp.float32
    )
    grad_value = jnp.einsum("hfs,fhd->shd", rounded, cot_heads, preferred_element_type=jnp.float32)
    grad_query = grad_query.reshape(frame_count, inner_width).astype(jnp.bfloat16)
    grad_terms = jnp.concatenate(
        [grad_key.reshape(key_span, inner_width), grad_value.reshape(key_span, inner_width)], axis=1
    )
    return (context, grad_query, grad_terms)


def weight_gradient(frame_rows, grad_all):
    frame_count, model_width = frame_rows.shape
    grad_width = grad_all.shape[1]
    calls = lax.axis_size(CALLS)
    pair = lax.axis_size("cc")
    spread = lax.axis_size(CALLS[:2])
    ring = lax.axis_size("cx")
    group = lax.axis_size("cy")
    ctx = ring * group
    block_rows = model_width // calls
    block_cols = grad_width // ctx
    col_factor = grad_all.reshape(frame_count, ring, group, block_cols).transpose(2, 0, 1, 3)
    col_factor = col_factor.reshape(group, frame_count, ring * block_cols)
    row_factor = jnp.broadcast_to(frame_rows[None], (group, frame_count, model_width))
    sent = jnp.concatenate([row_factor, col_factor], axis=2)
    got = lax.all_to_all(sent, "cy", 0, 0, tiled=True)
    row_pieces = got[..., :model_width].reshape(group, frame_count, spread, pair, block_rows)
    col_pieces = got[..., model_width:].reshape(group, frame_count, ring, block_cols)
    tile = jnp.einsum(
        "sfnha,sfxb->hxnab", row_pieces, col_pieces, preferred_element_type=jnp.float32
    ).reshape(pair, ring, spread, block_rows * block_cols)
    core = lax.axis_index("cc")
    keep = lax.dynamic_index_in_dim(tile, core, 0, keepdims=False)
    send = lax.dynamic_index_in_dim(tile, pair - 1 - core, 0, keepdims=False)
    half = keep + lax.ppermute(send, "cc", [(0, 1), (1, 0)])
    part = jnp.sum(lax.all_to_all(half, "cx", 0, 0, tiled=True), axis=0)
    summed = jnp.sum(lax.all_to_all(part, CALLS[:2], 0, 0, tiled=True), axis=0)
    return summed.reshape(block_rows, block_cols)


def body(frames_in, w_qkv, out_grad, lengths):
    frame_rows = frames_in[0]
    frame_count, model_width = frame_rows.shape
    inner_width = w_qkv.shape[1] // 3
    window = WIN
    offset = lax.axis_index(CTX) * frame_count
    length_now = lengths[0]
    qkv = jnp.dot(frame_rows, w_qkv, preferred_element_type=jnp.float32).astype(jnp.bfloat16)
    queries = qkv[:, :inner_width]
    key_value = with_halo(qkv[:, inner_width:], ((CTX, 0),), window)
    query_pos = offset + jnp.arange(frame_count, dtype=jnp.int32)
    key_pos = offset - window + jnp.arange(frame_count + 2 * window, dtype=jnp.int32)
    allowed = band_mask(query_pos, key_pos, length_now)
    live_rows = query_pos < length_now
    living = live_rows.astype(jnp.float32)
    cotangent = jnp.where(live_rows[:, None], out_grad[0], jnp.zeros_like(out_grad[0]))
    context, grad_query, grad_terms = attend(queries, key_value, cotangent, allowed, living)
    own_part = grad_terms[window : window + frame_count]
    rim_part = jnp.concatenate(
        [grad_terms[:window], grad_terms[window + frame_count :]], axis=0
    ).astype(jnp.bfloat16)
    returned = with_halo(rim_part, ((CTX, 0),), window)
    from_left = returned[:window].astype(jnp.float32)
    from_right = returned[3 * window :].astype(jnp.float32)
    summed = own_part + from_left
    summed = summed + from_right
    grad_kv = summed.astype(jnp.bfloat16)
    grad_all = jnp.concatenate([grad_query, grad_kv], axis=1)
    in_grad = lax.dot_general(
        grad_all, w_qkv, (((1,), (1,)), ((), ())), preferred_element_type=jnp.float32
    ).astype(jnp.bfloat16)
    weight_grad = weight_gradient(frame_rows, grad_all)
    return (context[None], in_grad[None], weight_grad)


def solution(mesh):
    calls, ctx = mesh.devices.shape
    pair = 2
    group = 4
    shape = (2, calls // (2 * pair), pair, ctx // group, group)
    fine = Mesh(mesh.devices.reshape(shape), CALLS + CTX)
    frames = P(CALLS, CTX, None)
    in_specs = (frames, P(), frames, P(CALLS))
    out_specs = (frames, frames, P(CALLS, CTX))
    return jax.shard_map(body, mesh=fine, in_specs=in_specs, out_specs=out_specs, check_vma=False)
```

```python
import math

import jax
import jax.numpy as jnp
from jax import lax
from jax.sharding import Mesh, PartitionSpec as P

HEADS = 4
WIN = 128
CALLS = ("ch", "cz", "cc")
CTX = ("cx", "cy")


def with_halo(cells, sides, width):
    for axis, dim in sides:
        count = lax.axis_size(axis)
        ends = count - 1
        head = lax.slice_in_dim(cells, 0, width, axis=dim)
        tail = lax.slice_in_dim(cells, cells.shape[dim] - width, cells.shape[dim], axis=dim)
        cells = jnp.concatenate(
            [
                lax.ppermute(tail, axis, [(i, (i + 1) % count) for i in range(ends)]),
                cells,
                lax.ppermute(head, axis, [((i + 1) % count, i) for i in range(ends)]),
            ],
            axis=dim,
        )
    return cells


def band_mask(query_pos, key_pos, length_now):
    gap = jnp.abs(query_pos[:, None] - key_pos[None, :])
    inside = (gap <= WIN) & (key_pos[None, :] >= 0) & (key_pos[None, :] < length_now)
    return inside | (query_pos[:, None] == key_pos[None, :])


def attend(queries, key_value, cotangent, allowed, living):
    frame_count, inner_width = queries.shape
    head_size = inner_width // HEADS
    key_span = key_value.shape[0]
    factor = 1.0 / math.sqrt(head_size)
    query_heads = queries.reshape(frame_count, HEADS, head_size)
    key_heads = key_value[:, :inner_width].reshape(key_span, HEADS, head_size)
    value_heads = key_value[:, inner_width:].reshape(key_span, HEADS, head_size)
    cot_heads = cotangent.reshape(frame_count, HEADS, head_size)
    scores = (
        jnp.einsum("fhd,shd->hfs", query_heads, key_heads, preferred_element_type=jnp.float32)
        * factor
    )
    scores = jnp.where(allowed[None], scores, -jnp.inf)
    maxima = jnp.max(scores, axis=-1, keepdims=True)
    shifted = jnp.exp(scores - maxima)
    totals = jnp.sum(shifted, axis=-1, keepdims=True)
    weights = shifted / totals
    rounded = weights.astype(jnp.bfloat16)
    context = jnp.einsum("hfs,shd->fhd", rounded, value_heads, preferred_element_type=jnp.float32)
    context = (
        (context * living[:, None, None]).reshape(frame_count, inner_width).astype(jnp.bfloat16)
    )
    grad_probs = jnp.einsum(
        "fhd,shd->hfs", cot_heads, value_heads, preferred_element_type=jnp.float32
    )
    centre_term = jnp.sum(grad_probs * weights, axis=-1, keepdims=True)
    grad_scores = (weights * (grad_probs - centre_term) * factor).astype(jnp.bfloat16)
    grad_query = jnp.einsum(
        "hfs,shd->fhd", grad_scores, key_heads, preferred_element_type=jnp.float32
    )
    grad_key = jnp.einsum(
        "hfs,fhd->shd", grad_scores, query_heads, preferred_element_type=jnp.float32
    )
    grad_value = jnp.einsum("hfs,fhd->shd", rounded, cot_heads, preferred_element_type=jnp.float32)
    grad_query = grad_query.reshape(frame_count, inner_width).astype(jnp.bfloat16)
    grad_terms = jnp.concatenate(
        [grad_key.reshape(key_span, inner_width), grad_value.reshape(key_span, inner_width)], axis=1
    )
    return (context, grad_query, grad_terms)


def weight_gradient(frame_rows, grad_all):
    frame_count, model_width = frame_rows.shape
    grad_width = grad_all.shape[1]
    calls = lax.axis_size(CALLS)
    pair = lax.axis_size("cc")
    spread = lax.axis_size(CALLS[:2])
    ring = lax.axis_size("cx")
    group = lax.axis_size("cy")
    ctx = ring * group
    block_rows = model_width // calls
    block_cols = grad_width // ctx
    col_factor = grad_all.reshape(frame_count, ring, group, block_cols).transpose(2, 0, 1, 3)
    col_factor = col_factor.reshape(group, frame_count, ring * block_cols)
    row_factor = jnp.broadcast_to(frame_rows[None], (group, frame_count, model_width))
    sent = jnp.concatenate([row_factor, col_factor], axis=2)
    got = lax.all_to_all(sent, "cy", 0, 0, tiled=True)
    tile = jnp.einsum(
        "sfr,sfc->rc", got[..., :model_width], got[..., model_width:],
        preferred_element_type=jnp.float32,
    ).reshape(spread, pair, block_rows, ring * block_cols)
    core = lax.axis_index("cc")
    keep = lax.dynamic_index_in_dim(tile, core, 1, keepdims=False)
    send = lax.dynamic_index_in_dim(tile, pair - 1 - core, 1, keepdims=False)
    half = keep + lax.ppermute(send, "cc", [(0, 1), (1, 0)])
    half = half.reshape(spread, block_rows, ring, block_cols)
    part = jnp.sum(lax.all_to_all(half, "cx", 2, 2, tiled=True), axis=2)
    part = part.reshape(spread, block_rows * block_cols)
    summed = jnp.sum(lax.all_to_all(part, CALLS[:2], 0, 0, tiled=True), axis=0)
    return summed.reshape(block_rows, block_cols)


def body(frames_in, w_qkv, out_grad, lengths):
    frame_rows = frames_in[0]
    frame_count, model_width = frame_rows.shape
    inner_width = w_qkv.shape[1] // 3
    window = WIN
    offset = lax.axis_index(CTX) * frame_count
    length_now = lengths[0]
    qkv = jnp.dot(frame_rows, w_qkv, preferred_element_type=jnp.float32).astype(jnp.bfloat16)
    queries = qkv[:, :inner_width]
    key_value = with_halo(qkv[:, inner_width:], ((CTX, 0),), window)
    query_pos = offset + jnp.arange(frame_count, dtype=jnp.int32)
    key_pos = offset - window + jnp.arange(frame_count + 2 * window, dtype=jnp.int32)
    allowed = band_mask(query_pos, key_pos, length_now)
    live_rows = query_pos < length_now
    living = live_rows.astype(jnp.float32)
    cotangent = jnp.where(live_rows[:, None], out_grad[0], jnp.zeros_like(out_grad[0]))
    context, grad_query, grad_terms = attend(queries, key_value, cotangent, allowed, living)
    own_part = grad_terms[window : window + frame_count]
    rim_part = jnp.concatenate(
        [grad_terms[:window], grad_terms[window + frame_count :]], axis=0
    ).astype(jnp.bfloat16)
    returned = with_halo(rim_part, ((CTX, 0),), window)
    from_left = returned[:window].astype(jnp.float32)
    from_right = returned[3 * window :].astype(jnp.float32)
    summed = own_part + from_left
    summed = summed + from_right
    grad_kv = summed.astype(jnp.bfloat16)
    grad_all = jnp.concatenate([grad_query, grad_kv], axis=1)
    in_grad = lax.dot_general(
        grad_all, w_qkv, (((1,), (1,)), ((), ())), preferred_element_type=jnp.float32
    ).astype(jnp.bfloat16)
    weight_grad = weight_gradient(frame_rows, grad_all)
    return (context[None], in_grad[None], weight_grad)


def solution(mesh):
    calls, ctx = mesh.devices.shape
    pair = 2
    group = 4
    shape = (2, calls // (2 * pair), pair, ctx // group, group)
    fine = Mesh(mesh.devices.reshape(shape), CALLS + CTX)
    frames = P(CALLS, CTX, None)
    in_specs = (frames, P(), frames, P(CALLS))
    out_specs = (frames, frames, P(CALLS, CTX))
    return jax.shard_map(body, mesh=fine, in_specs=in_specs, out_specs=out_specs, check_vma=False)
```

```python
import math

import jax
import jax.numpy as jnp
from jax import lax
from jax.sharding import Mesh, PartitionSpec as P

HEADS = 4
WIN = 128
CALLS = ("ch", "cz", "cc")
CTX = ("cx", "cy")


def with_halo(cells, sides, width):
    for axis, dim in sides:
        count = lax.axis_size(axis)
        ends = count - 1
        head = lax.slice_in_dim(cells, 0, width, axis=dim)
        tail = lax.slice_in_dim(cells, cells.shape[dim] - width, cells.shape[dim], axis=dim)
        cells = jnp.concatenate(
            [
                lax.ppermute(tail, axis, [(i, (i + 1) % count) for i in range(ends)]),
                cells,
                lax.ppermute(head, axis, [((i + 1) % count, i) for i in range(ends)]),
            ],
            axis=dim,
        )
    return cells


def band_mask(query_pos, key_pos, length_now):
    gap = jnp.abs(query_pos[:, None] - key_pos[None, :])
    inside = (gap <= WIN) & (key_pos[None, :] >= 0) & (key_pos[None, :] < length_now)
    return inside | (query_pos[:, None] == key_pos[None, :])


def attend(queries, key_value, cotangent, allowed, living):
    frame_count, inner_width = queries.shape
    head_size = inner_width // HEADS
    key_span = key_value.shape[0]
    factor = 1.0 / math.sqrt(head_size)
    query_heads = queries.reshape(frame_count, HEADS, head_size)
    key_heads = key_value[:, :inner_width].reshape(key_span, HEADS, head_size)
    value_heads = key_value[:, inner_width:].reshape(key_span, HEADS, head_size)
    cot_heads = cotangent.reshape(frame_count, HEADS, head_size)
    scores = (
        jnp.einsum("fhd,shd->hfs", query_heads, key_heads, preferred_element_type=jnp.float32)
        * factor
    )
    scores = jnp.where(allowed[None], scores, -jnp.inf)
    maxima = jnp.max(scores, axis=-1, keepdims=True)
    shifted = jnp.exp(scores - maxima)
    totals = jnp.sum(shifted, axis=-1, keepdims=True)
    weights = shifted / totals
    rounded = weights.astype(jnp.bfloat16)
    context = jnp.einsum("hfs,shd->fhd", rounded, value_heads, preferred_element_type=jnp.float32)
    context = (
        (context * living[:, None, None]).reshape(frame_count, inner_width).astype(jnp.bfloat16)
    )
    grad_probs = jnp.einsum(
        "fhd,shd->hfs", cot_heads, value_heads, preferred_element_type=jnp.float32
    )
    centre_term = jnp.sum(grad_probs * weights, axis=-1, keepdims=True)
    grad_scores = (weights * (grad_probs - centre_term) * factor).astype(jnp.bfloat16)
    grad_query = jnp.einsum(
        "hfs,shd->fhd", grad_scores, key_heads, preferred_element_type=jnp.float32
    )
    grad_key = jnp.einsum(
        "hfs,fhd->shd", grad_scores, query_heads, preferred_element_type=jnp.float32
    )
    grad_value = jnp.einsum("hfs,fhd->shd", rounded, cot_heads, preferred_element_type=jnp.float32)
    grad_query = grad_query.reshape(frame_count, inner_width).astype(jnp.bfloat16)
    grad_terms = jnp.concatenate(
        [grad_key.reshape(key_span, inner_width), grad_value.reshape(key_span, inner_width)], axis=1
    )
    return (context, grad_query, grad_terms)


def weight_gradient(frame_rows, grad_all):
    frame_count, model_width = frame_rows.shape
    grad_width = grad_all.shape[1]
    calls = lax.axis_size(CALLS)
    pair = lax.axis_size("cc")
    spread = lax.axis_size(CALLS[:2])
    ring = lax.axis_size("cx")
    group = lax.axis_size("cy")
    ctx = ring * group
    block_rows = model_width // calls
    block_cols = grad_width // ctx
    col_factor = grad_all.reshape(frame_count, ring, group, block_cols).transpose(2, 0, 1, 3)
    col_factor = col_factor.reshape(group, frame_count, ring * block_cols)
    row_factor = jnp.broadcast_to(frame_rows[None], (group, frame_count, model_width))
    sent = jnp.concatenate([row_factor, col_factor], axis=2)
    got = lax.all_to_all(sent, "cy", 0, 0, tiled=True)
    row_pieces = got[..., :model_width].reshape(group, frame_count, spread, pair, block_rows)
    col_pieces = got[..., model_width:].reshape(group, frame_count, ring, block_cols)
    halves = [
        jnp.einsum(
            "sfna,sfxb->xnab", row_pieces[:, :, :, h], col_pieces, preferred_element_type=jnp.float32
        ).reshape(ring, spread, block_rows * block_cols)
        for h in range(pair)
    ]
    core = lax.axis_index("cc")
    keep = jnp.where(core == 0, halves[0], halves[1])
    send = jnp.where(core == 0, halves[1], halves[0])
    half = keep + lax.ppermute(send, "cc", [(0, 1), (1, 0)])
    part = jnp.sum(lax.all_to_all(half, "cx", 0, 0, tiled=True), axis=0)
    summed = jnp.sum(lax.all_to_all(part, CALLS[:2], 0, 0, tiled=True), axis=0)
    return summed.reshape(block_rows, block_cols)


def body(frames_in, w_qkv, out_grad, lengths):
    frame_rows = frames_in[0]
    frame_count, model_width = frame_rows.shape
    inner_width = w_qkv.shape[1] // 3
    window = WIN
    offset = lax.axis_index(CTX) * frame_count
    length_now = lengths[0]
    qkv = jnp.dot(frame_rows, w_qkv, preferred_element_type=jnp.float32).astype(jnp.bfloat16)
    queries = qkv[:, :inner_width]
    key_value = with_halo(qkv[:, inner_width:], ((CTX, 0),), window)
    query_pos = offset + jnp.arange(frame_count, dtype=jnp.int32)
    key_pos = offset - window + jnp.arange(frame_count + 2 * window, dtype=jnp.int32)
    allowed = band_mask(query_pos, key_pos, length_now)
    live_rows = query_pos < length_now
    living = live_rows.astype(jnp.float32)
    cotangent = jnp.where(live_rows[:, None], out_grad[0], jnp.zeros_like(out_grad[0]))
    context, grad_query, grad_terms = attend(queries, key_value, cotangent, allowed, living)
    own_part = grad_terms[window : window + frame_count]
    rim_part = jnp.concatenate(
        [grad_terms[:window], grad_terms[window + frame_count :]], axis=0
    ).astype(jnp.bfloat16)
    returned = with_halo(rim_part, ((CTX, 0),), window)
    from_left = returned[:window].astype(jnp.float32)
    from_right = returned[3 * window :].astype(jnp.float32)
    summed = own_part + from_left
    summed = summed + from_right
    grad_kv = summed.astype(jnp.bfloat16)
    grad_all = jnp.concatenate([grad_query, grad_kv], axis=1)
    in_grad = lax.dot_general(
        grad_all, w_qkv, (((1,), (1,)), ((), ())), preferred_element_type=jnp.float32
    ).astype(jnp.bfloat16)
    weight_grad = weight_gradient(frame_rows, grad_all)
    return (context[None], in_grad[None], weight_grad)


def solution(mesh):
    calls, ctx = mesh.devices.shape
    pair = 2
    group = 4
    shape = (2, calls // (2 * pair), pair, ctx // group, group)
    fine = Mesh(mesh.devices.reshape(shape), CALLS + CTX)
    frames = P(CALLS, CTX, None)
    in_specs = (frames, P(), frames, P(CALLS))
    out_specs = (frames, frames, P(CALLS, CTX))
    return jax.shard_map(body, mesh=fine, in_specs=in_specs, out_specs=out_specs, check_vma=False)
```

```python
import math

import jax
import jax.numpy as jnp
from jax import lax
from jax.sharding import Mesh, PartitionSpec as P

HEADS = 4
WIN = 128
CALLS = ("ch", "cz", "cc")
CTX = ("cx", "cy")


def with_halo(cells, sides, width):
    for axis, dim in sides:
        count = lax.axis_size(axis)
        ends = count - 1
        head = lax.slice_in_dim(cells, 0, width, axis=dim)
        tail = lax.slice_in_dim(cells, cells.shape[dim] - width, cells.shape[dim], axis=dim)
        cells = jnp.concatenate(
            [
                lax.ppermute(tail, axis, [(i, (i + 1) % count) for i in range(ends)]),
                cells,
                lax.ppermute(head, axis, [((i + 1) % count, i) for i in range(ends)]),
            ],
            axis=dim,
        )
    return cells


def band_mask(query_pos, key_pos, length_now):
    gap = jnp.abs(query_pos[:, None] - key_pos[None, :])
    inside = (gap <= WIN) & (key_pos[None, :] >= 0) & (key_pos[None, :] < length_now)
    return inside | (query_pos[:, None] == key_pos[None, :])


def attend(queries, key_value, cotangent, allowed, living):
    frame_count, inner_width = queries.shape
    head_size = inner_width // HEADS
    key_span = key_value.shape[0]
    factor = 1.0 / math.sqrt(head_size)
    query_heads = queries.reshape(frame_count, HEADS, head_size)
    key_heads = key_value[:, :inner_width].reshape(key_span, HEADS, head_size)
    value_heads = key_value[:, inner_width:].reshape(key_span, HEADS, head_size)
    cot_heads = cotangent.reshape(frame_count, HEADS, head_size)
    scores = (
        jnp.einsum("fhd,shd->hfs", query_heads, key_heads, preferred_element_type=jnp.float32)
        * factor
    )
    scores = jnp.where(allowed[None], scores, -jnp.inf)
    maxima = jnp.max(scores, axis=-1, keepdims=True)
    shifted = jnp.exp(scores - maxima)
    totals = jnp.sum(shifted, axis=-1, keepdims=True)
    weights = shifted / totals
    rounded = weights.astype(jnp.bfloat16)
    context = jnp.einsum("hfs,shd->fhd", rounded, value_heads, preferred_element_type=jnp.float32)
    context = (
        (context * living[:, None, None]).reshape(frame_count, inner_width).astype(jnp.bfloat16)
    )
    grad_probs = jnp.einsum(
        "fhd,shd->hfs", cot_heads, value_heads, preferred_element_type=jnp.float32
    )
    centre_term = jnp.sum(grad_probs * weights, axis=-1, keepdims=True)
    grad_scores = (weights * (grad_probs - centre_term) * factor).astype(jnp.bfloat16)
    grad_query = jnp.einsum(
        "hfs,shd->fhd", grad_scores, key_heads, preferred_element_type=jnp.float32
    )
    grad_key = jnp.einsum(
        "hfs,fhd->shd", grad_scores, query_heads, preferred_element_type=jnp.float32
    )
    grad_value = jnp.einsum("hfs,fhd->shd", rounded, cot_heads, preferred_element_type=jnp.float32)
    grad_query = grad_query.reshape(frame_count, inner_width).astype(jnp.bfloat16)
    grad_terms = jnp.concatenate(
        [grad_key.reshape(key_span, inner_width), grad_value.reshape(key_span, inner_width)], axis=1
    )
    return (context, grad_query, grad_terms)


def weight_gradient(frame_rows, grad_all):
    frame_count, model_width = frame_rows.shape
    grad_width = grad_all.shape[1]
    calls = lax.axis_size(CALLS)
    pair = lax.axis_size("cc")
    spread = lax.axis_size(CALLS[:2])
    ring = lax.axis_size("cx")
    group = lax.axis_size("cy")
    ctx = ring * group
    block_rows = model_width // calls
    block_cols = grad_width // ctx
    col_factor = grad_all.reshape(frame_count, ring, group, block_cols).transpose(2, 0, 1, 3)
    col_factor = col_factor.reshape(group, frame_count, ring * block_cols)
    row_factor = jnp.broadcast_to(frame_rows[None], (group, frame_count, model_width))
    sent = jnp.concatenate([row_factor, col_factor], axis=2)
    got = lax.all_to_all(sent, "cy", 0, 0, tiled=True)
    row_pieces = got[..., :model_width].reshape(group, frame_count, spread, pair, block_rows)
    col_pieces = got[..., model_width:].reshape(group, frame_count, ring, block_cols)
    core = lax.axis_index("cc")
    keep, send = [
        jnp.einsum(
            "sfna,sfxb->xnab",
            lax.dynamic_index_in_dim(row_pieces, h, 3, keepdims=False),
            col_pieces,
            preferred_element_type=jnp.float32,
        ).reshape(ring, spread, block_rows * block_cols)
        for h in (core, pair - 1 - core)
    ]
    half = keep + lax.ppermute(send, "cc", [(0, 1), (1, 0)])
    part = jnp.sum(lax.all_to_all(half, "cx", 0, 0, tiled=True), axis=0)
    summed = jnp.sum(lax.all_to_all(part, CALLS[:2], 0, 0, tiled=True), axis=0)
    return summed.reshape(block_rows, block_cols)


def body(frames_in, w_qkv, out_grad, lengths):
    frame_rows = frames_in[0]
    frame_count, model_width = frame_rows.shape
    inner_width = w_qkv.shape[1] // 3
    window = WIN
    offset = lax.axis_index(CTX) * frame_count
    length_now = lengths[0]
    qkv = jnp.dot(frame_rows, w_qkv, preferred_element_type=jnp.float32).astype(jnp.bfloat16)
    queries = qkv[:, :inner_width]
    key_value = with_halo(qkv[:, inner_width:], ((CTX, 0),), window)
    query_pos = offset + jnp.arange(frame_count, dtype=jnp.int32)
    key_pos = offset - window + jnp.arange(frame_count + 2 * window, dtype=jnp.int32)
    allowed = band_mask(query_pos, key_pos, length_now)
    live_rows = query_pos < length_now
    living = live_rows.astype(jnp.float32)
    cotangent = jnp.where(live_rows[:, None], out_grad[0], jnp.zeros_like(out_grad[0]))
    context, grad_query, grad_terms = attend(queries, key_value, cotangent, allowed, living)
    own_part = grad_terms[window : window + frame_count]
    rim_part = jnp.concatenate(
        [grad_terms[:window], grad_terms[window + frame_count :]], axis=0
    ).astype(jnp.bfloat16)
    returned = with_halo(rim_part, ((CTX, 0),), window)
    from_left = returned[:window].astype(jnp.float32)
    from_right = returned[3 * window :].astype(jnp.float32)
    summed = own_part + from_left
    summed = summed + from_right
    grad_kv = summed.astype(jnp.bfloat16)
    grad_all = jnp.concatenate([grad_query, grad_kv], axis=1)
    in_grad = lax.dot_general(
        grad_all, w_qkv, (((1,), (1,)), ((), ())), preferred_element_type=jnp.float32
    ).astype(jnp.bfloat16)
    weight_grad = weight_gradient(frame_rows, grad_all)
    return (context[None], in_grad[None], weight_grad)


def solution(mesh):
    calls, ctx = mesh.devices.shape
    pair = 2
    group = 4
    shape = (2, calls // (2 * pair), pair, ctx // group, group)
    fine = Mesh(mesh.devices.reshape(shape), CALLS + CTX)
    frames = P(CALLS, CTX, None)
    in_specs = (frames, P(), frames, P(CALLS))
    out_specs = (frames, frames, P(CALLS, CTX))
    return jax.shard_map(body, mesh=fine, in_specs=in_specs, out_specs=out_specs, check_vma=False)
```

```python
import math

import jax
import jax.numpy as jnp
from jax import lax
from jax.sharding import Mesh, PartitionSpec as P

HEADS = 4
WIN = 128
CALLS = ("ch", "cz", "cc")
CTX = ("cx", "cy")


def with_halo(cells, sides, width):
    for axis, dim in sides:
        count = lax.axis_size(axis)
        ends = count - 1
        head = lax.slice_in_dim(cells, 0, width, axis=dim)
        tail = lax.slice_in_dim(cells, cells.shape[dim] - width, cells.shape[dim], axis=dim)
        cells = jnp.concatenate(
            [
                lax.ppermute(tail, axis, [(i, (i + 1) % count) for i in range(ends)]),
                cells,
                lax.ppermute(head, axis, [((i + 1) % count, i) for i in range(ends)]),
            ],
            axis=dim,
        )
    return cells


def band_mask(query_pos, key_pos, length_now):
    gap = jnp.abs(query_pos[:, None] - key_pos[None, :])
    inside = (gap <= WIN) & (key_pos[None, :] >= 0) & (key_pos[None, :] < length_now)
    return inside | (query_pos[:, None] == key_pos[None, :])


def attend(queries, key_value, cotangent, allowed, living):
    frame_count, inner_width = queries.shape
    head_size = inner_width // HEADS
    key_span = key_value.shape[0]
    factor = 1.0 / math.sqrt(head_size)
    query_heads = queries.reshape(frame_count, HEADS, head_size)
    key_heads = key_value[:, :inner_width].reshape(key_span, HEADS, head_size)
    value_heads = key_value[:, inner_width:].reshape(key_span, HEADS, head_size)
    cot_heads = cotangent.reshape(frame_count, HEADS, head_size)
    scores = (
        jnp.einsum("fhd,shd->hfs", query_heads, key_heads, preferred_element_type=jnp.float32)
        * factor
    )
    scores = jnp.where(allowed[None], scores, -jnp.inf)
    maxima = jnp.max(scores, axis=-1, keepdims=True)
    shifted = jnp.exp(scores - maxima)
    totals = jnp.sum(shifted, axis=-1, keepdims=True)
    weights = shifted / totals
    rounded = weights.astype(jnp.bfloat16)
    context = jnp.einsum("hfs,shd->fhd", rounded, value_heads, preferred_element_type=jnp.float32)
    context = (
        (context * living[:, None, None]).reshape(frame_count, inner_width).astype(jnp.bfloat16)
    )
    grad_probs = jnp.einsum(
        "fhd,shd->hfs", cot_heads, value_heads, preferred_element_type=jnp.float32
    )
    centre_term = jnp.sum(grad_probs * weights, axis=-1, keepdims=True)
    grad_scores = (weights * (grad_probs - centre_term) * factor).astype(jnp.bfloat16)
    grad_query = jnp.einsum(
        "hfs,shd->fhd", grad_scores, key_heads, preferred_element_type=jnp.float32
    )
    grad_key = jnp.einsum(
        "hfs,fhd->shd", grad_scores, query_heads, preferred_element_type=jnp.float32
    )
    grad_value = jnp.einsum("hfs,fhd->shd", rounded, cot_heads, preferred_element_type=jnp.float32)
    grad_query = grad_query.reshape(frame_count, inner_width).astype(jnp.bfloat16)
    grad_terms = jnp.concatenate(
        [grad_key.reshape(key_span, inner_width), grad_value.reshape(key_span, inner_width)], axis=1
    )
    return (context, grad_query, grad_terms)


def weight_gradient(frame_rows, grad_all):
    frame_count, model_width = frame_rows.shape
    grad_width = grad_all.shape[1]
    calls = lax.axis_size(CALLS)
    pair = lax.axis_size("cc")
    spread = lax.axis_size(CALLS[:2])
    ring = lax.axis_size("cx")
    group = lax.axis_size("cy")
    ctx = ring * group
    block_rows = model_width // calls
    block_cols = grad_width // ctx
    col_factor = grad_all.reshape(frame_count, ring, group, block_cols).transpose(2, 0, 1, 3)
    col_factor = col_factor.reshape(group, frame_count, ring * block_cols)
    row_factor = jnp.broadcast_to(frame_rows[None], (group, frame_count, model_width))
    got_rows = lax.all_to_all(row_factor, "cy", 0, 0, tiled=True)
    got_cols = lax.all_to_all(col_factor, "cy", 0, 0, tiled=True)
    row_pieces = got_rows.reshape(group, frame_count, spread, pair, block_rows)
    col_pieces = got_cols.reshape(group, frame_count, ring, block_cols)
    halves = [
        jnp.einsum(
            "sfna,sfxb->xnab", row_pieces[:, :, :, h], col_pieces, preferred_element_type=jnp.float32
        ).reshape(ring, spread, block_rows * block_cols)
        for h in range(pair)
    ]
    core = lax.axis_index("cc")
    keep = jnp.where(core == 0, halves[0], halves[1])
    send = jnp.where(core == 0, halves[1], halves[0])
    half = keep + lax.ppermute(send, "cc", [(0, 1), (1, 0)])
    part = jnp.sum(lax.all_to_all(half, "cx", 0, 0, tiled=True), axis=0)
    summed = jnp.sum(lax.all_to_all(part, CALLS[:2], 0, 0, tiled=True), axis=0)
    return summed.reshape(block_rows, block_cols)


def body(frames_in, w_qkv, out_grad, lengths):
    frame_rows = frames_in[0]
    frame_count, model_width = frame_rows.shape
    inner_width = w_qkv.shape[1] // 3
    window = WIN
    offset = lax.axis_index(CTX) * frame_count
    length_now = lengths[0]
    qkv = jnp.dot(frame_rows, w_qkv, preferred_element_type=jnp.float32).astype(jnp.bfloat16)
    queries = qkv[:, :inner_width]
    key_value = with_halo(qkv[:, inner_width:], ((CTX, 0),), window)
    query_pos = offset + jnp.arange(frame_count, dtype=jnp.int32)
    key_pos = offset - window + jnp.arange(frame_count + 2 * window, dtype=jnp.int32)
    allowed = band_mask(query_pos, key_pos, length_now)
    live_rows = query_pos < length_now
    living = live_rows.astype(jnp.float32)
    cotangent = jnp.where(live_rows[:, None], out_grad[0], jnp.zeros_like(out_grad[0]))
    context, grad_query, grad_terms = attend(queries, key_value, cotangent, allowed, living)
    own_part = grad_terms[window : window + frame_count]
    rim_part = jnp.concatenate(
        [grad_terms[:window], grad_terms[window + frame_count :]], axis=0
    ).astype(jnp.bfloat16)
    returned = with_halo(rim_part, ((CTX, 0),), window)
    from_left = returned[:window].astype(jnp.float32)
    from_right = returned[3 * window :].astype(jnp.float32)
    summed = own_part + from_left
    summed = summed + from_right
    grad_kv = summed.astype(jnp.bfloat16)
    grad_all = jnp.concatenate([grad_query, grad_kv], axis=1)
    in_grad = lax.dot_general(
        grad_all, w_qkv, (((1,), (1,)), ((), ())), preferred_element_type=jnp.float32
    ).astype(jnp.bfloat16)
    weight_grad = weight_gradient(frame_rows, grad_all)
    return (context[None], in_grad[None], weight_grad)


def solution(mesh):
    calls, ctx = mesh.devices.shape
    pair = 2
    group = 4
    shape = (2, calls // (2 * pair), pair, ctx // group, group)
    fine = Mesh(mesh.devices.reshape(shape), CALLS + CTX)
    frames = P(CALLS, CTX, None)
    in_specs = (frames, P(), frames, P(CALLS))
    out_specs = (frames, frames, P(CALLS, CTX))
    return jax.shard_map(body, mesh=fine, in_specs=in_specs, out_specs=out_specs, check_vma=False)
```

```python
import math

import jax
import jax.numpy as jnp
from jax import lax
from jax.sharding import Mesh, PartitionSpec as P

HEADS = 4
WIN = 128
CALLS = ("ch", "cz", "cc")
CTX = ("cx", "cy")


def with_halo(cells, sides, width):
    for axis, dim in sides:
        count = lax.axis_size(axis)
        ends = count - 1
        head = lax.slice_in_dim(cells, 0, width, axis=dim)
        tail = lax.slice_in_dim(cells, cells.shape[dim] - width, cells.shape[dim], axis=dim)
        cells = jnp.concatenate(
            [
                lax.ppermute(tail, axis, [(i, (i + 1) % count) for i in range(ends)]),
                cells,
                lax.ppermute(head, axis, [((i + 1) % count, i) for i in range(ends)]),
            ],
            axis=dim,
        )
    return cells


def band_mask(query_pos, key_pos, length_now):
    gap = jnp.abs(query_pos[:, None] - key_pos[None, :])
    inside = (gap <= WIN) & (key_pos[None, :] >= 0) & (key_pos[None, :] < length_now)
    return inside | (query_pos[:, None] == key_pos[None, :])


def attend(queries, key_value, cotangent, allowed, living):
    frame_count, inner_width = queries.shape
    head_size = inner_width // HEADS
    key_span = key_value.shape[0]
    factor = 1.0 / math.sqrt(head_size)
    query_heads = queries.reshape(frame_count, HEADS, head_size)
    key_heads = key_value[:, :inner_width].reshape(key_span, HEADS, head_size)
    value_heads = key_value[:, inner_width:].reshape(key_span, HEADS, head_size)
    cot_heads = cotangent.reshape(frame_count, HEADS, head_size)
    scores = (
        jnp.einsum("fhd,shd->hfs", query_heads, key_heads, preferred_element_type=jnp.float32)
        * factor
    )
    scores = jnp.where(allowed[None], scores, -jnp.inf)
    maxima = jnp.max(scores, axis=-1, keepdims=True)
    shifted = jnp.exp(scores - maxima)
    totals = jnp.sum(shifted, axis=-1, keepdims=True)
    weights = shifted / totals
    rounded = weights.astype(jnp.bfloat16)
    context = jnp.einsum("hfs,shd->fhd", rounded, value_heads, preferred_element_type=jnp.float32)
    context = (
        (context * living[:, None, None]).reshape(frame_count, inner_width).astype(jnp.bfloat16)
    )
    grad_probs = jnp.einsum(
        "fhd,shd->hfs", cot_heads, value_heads, preferred_element_type=jnp.float32
    )
    centre_term = jnp.sum(grad_probs * weights, axis=-1, keepdims=True)
    grad_scores = (weights * (grad_probs - centre_term) * factor).astype(jnp.bfloat16)
    grad_query = jnp.einsum(
        "hfs,shd->fhd", grad_scores, key_heads, preferred_element_type=jnp.float32
    )
    grad_key = jnp.einsum(
        "hfs,fhd->shd", grad_scores, query_heads, preferred_element_type=jnp.float32
    )
    grad_value = jnp.einsum("hfs,fhd->shd", rounded, cot_heads, preferred_element_type=jnp.float32)
    grad_query = grad_query.reshape(frame_count, inner_width).astype(jnp.bfloat16)
    grad_terms = jnp.concatenate(
        [grad_key.reshape(key_span, inner_width), grad_value.reshape(key_span, inner_width)], axis=1
    )
    return (context, grad_query, grad_terms)


def weight_gradient(frame_rows, grad_all):
    frame_count, model_width = frame_rows.shape
    grad_width = grad_all.shape[1]
    calls = lax.axis_size(CALLS)
    pair = lax.axis_size("cc")
    spread = lax.axis_size(CALLS[:2])
    ring = lax.axis_size("cx")
    group = lax.axis_size("cy")
    ctx = ring * group
    block_rows = model_width // calls
    block_cols = grad_width // ctx
    col_factor = grad_all.reshape(frame_count, ring, group, block_cols).transpose(2, 0, 1, 3)
    col_factor = col_factor.reshape(group, frame_count, ring * block_cols)
    core = lax.axis_index("cc")
    own_rows = frame_rows.reshape(frame_count, spread, pair, block_rows)
    own_rows = jnp.where(core == 0, own_rows, own_rows[:, :, ::-1])
    row_factor = jnp.broadcast_to(own_rows.reshape(1, frame_count, -1), (group, frame_count, model_width))
    got_rows = lax.all_to_all(row_factor, "cy", 0, 0, tiled=True)
    got_cols = lax.all_to_all(col_factor, "cy", 0, 0, tiled=True)
    row_pieces = got_rows.reshape(group, frame_count, spread, pair, block_rows)
    col_pieces = got_cols.reshape(group, frame_count, ring, block_cols)
    keep, send = [
        jnp.einsum(
            "sfna,sfxb->xnab", row_pieces[:, :, :, h], col_pieces, preferred_element_type=jnp.float32
        ).reshape(ring, spread, block_rows * block_cols)
        for h in range(pair)
    ]
    half = keep + lax.ppermute(send, "cc", [(0, 1), (1, 0)])
    part = jnp.sum(lax.all_to_all(half, "cx", 0, 0, tiled=True), axis=0)
    summed = jnp.sum(lax.all_to_all(part, CALLS[:2], 0, 0, tiled=True), axis=0)
    return summed.reshape(block_rows, block_cols)


def body(frames_in, w_qkv, out_grad, lengths):
    frame_rows = frames_in[0]
    frame_count, model_width = frame_rows.shape
    inner_width = w_qkv.shape[1] // 3
    window = WIN
    offset = lax.axis_index(CTX) * frame_count
    length_now = lengths[0]
    qkv = jnp.dot(frame_rows, w_qkv, preferred_element_type=jnp.float32).astype(jnp.bfloat16)
    queries = qkv[:, :inner_width]
    key_value = with_halo(qkv[:, inner_width:], ((CTX, 0),), window)
    query_pos = offset + jnp.arange(frame_count, dtype=jnp.int32)
    key_pos = offset - window + jnp.arange(frame_count + 2 * window, dtype=jnp.int32)
    allowed = band_mask(query_pos, key_pos, length_now)
    live_rows = query_pos < length_now
    living = live_rows.astype(jnp.float32)
    cotangent = jnp.where(live_rows[:, None], out_grad[0], jnp.zeros_like(out_grad[0]))
    context, grad_query, grad_terms = attend(queries, key_value, cotangent, allowed, living)
    own_part = grad_terms[window : window + frame_count]
    rim_part = jnp.concatenate(
        [grad_terms[:window], grad_terms[window + frame_count :]], axis=0
    ).astype(jnp.bfloat16)
    returned = with_halo(rim_part, ((CTX, 0),), window)
    from_left = returned[:window].astype(jnp.float32)
    from_right = returned[3 * window :].astype(jnp.float32)
    summed = own_part + from_left
    summed = summed + from_right
    grad_kv = summed.astype(jnp.bfloat16)
    grad_all = jnp.concatenate([grad_query, grad_kv], axis=1)
    in_grad = lax.dot_general(
        grad_all, w_qkv, (((1,), (1,)), ((), ())), preferred_element_type=jnp.float32
    ).astype(jnp.bfloat16)
    weight_grad = weight_gradient(frame_rows, grad_all)
    return (context[None], in_grad[None], weight_grad)


def solution(mesh):
    calls, ctx = mesh.devices.shape
    pair = 2
    group = 4
    shape = (2, calls // (2 * pair), pair, ctx // group, group)
    fine = Mesh(mesh.devices.reshape(shape), CALLS + CTX)
    frames = P(CALLS, CTX, None)
    in_specs = (frames, P(), frames, P(CALLS))
    out_specs = (frames, frames, P(CALLS, CTX))
    return jax.shard_map(body, mesh=fine, in_specs=in_specs, out_specs=out_specs, check_vma=False)
```

```python
import math

import jax
import jax.numpy as jnp
from jax import lax
from jax.sharding import Mesh, PartitionSpec as P

HEADS = 4
WIN = 128
CALLS = ("ch", "cz", "cc")
CTX = ("cx", "cy")


def with_halo(cells, sides, width):
    for axis, dim in sides:
        count = lax.axis_size(axis)
        ends = count - 1
        head = lax.slice_in_dim(cells, 0, width, axis=dim)
        tail = lax.slice_in_dim(cells, cells.shape[dim] - width, cells.shape[dim], axis=dim)
        cells = jnp.concatenate(
            [
                lax.ppermute(tail, axis, [(i, (i + 1) % count) for i in range(ends)]),
                cells,
                lax.ppermute(head, axis, [((i + 1) % count, i) for i in range(ends)]),
            ],
            axis=dim,
        )
    return cells


def band_mask(query_pos, key_pos, length_now):
    gap = jnp.abs(query_pos[:, None] - key_pos[None, :])
    inside = (gap <= WIN) & (key_pos[None, :] >= 0) & (key_pos[None, :] < length_now)
    return inside | (query_pos[:, None] == key_pos[None, :])


def attend(queries, key_value, cotangent, allowed, living):
    frame_count, inner_width = queries.shape
    head_size = inner_width // HEADS
    key_span = key_value.shape[0]
    factor = 1.0 / math.sqrt(head_size)
    query_heads = queries.reshape(frame_count, HEADS, head_size)
    key_heads = key_value[:, :inner_width].reshape(key_span, HEADS, head_size)
    value_heads = key_value[:, inner_width:].reshape(key_span, HEADS, head_size)
    cot_heads = cotangent.reshape(frame_count, HEADS, head_size)
    scores = (
        jnp.einsum("fhd,shd->hfs", query_heads, key_heads, preferred_element_type=jnp.float32)
        * factor
    )
    scores = jnp.where(allowed[None], scores, -jnp.inf)
    maxima = jnp.max(scores, axis=-1, keepdims=True)
    shifted = jnp.exp(scores - maxima)
    totals = jnp.sum(shifted, axis=-1, keepdims=True)
    weights = shifted / totals
    rounded = weights.astype(jnp.bfloat16)
    context = jnp.einsum("hfs,shd->fhd", rounded, value_heads, preferred_element_type=jnp.float32)
    context = (
        (context * living[:, None, None]).reshape(frame_count, inner_width).astype(jnp.bfloat16)
    )
    grad_probs = jnp.einsum(
        "fhd,shd->hfs", cot_heads, value_heads, preferred_element_type=jnp.float32
    )
    centre_term = jnp.sum(grad_probs * weights, axis=-1, keepdims=True)
    grad_scores = (weights * (grad_probs - centre_term) * factor).astype(jnp.bfloat16)
    grad_query = jnp.einsum(
        "hfs,shd->fhd", grad_scores, key_heads, preferred_element_type=jnp.float32
    )
    grad_key = jnp.einsum(
        "hfs,fhd->shd", grad_scores, query_heads, preferred_element_type=jnp.float32
    )
    grad_value = jnp.einsum("hfs,fhd->shd", rounded, cot_heads, preferred_element_type=jnp.float32)
    grad_query = grad_query.reshape(frame_count, inner_width).astype(jnp.bfloat16)
    grad_terms = jnp.concatenate(
        [grad_key.reshape(key_span, inner_width), grad_value.reshape(key_span, inner_width)], axis=1
    )
    return (context, grad_query, grad_terms)


def weight_gradient(frame_rows, grad_all):
    frame_count, model_width = frame_rows.shape
    grad_width = grad_all.shape[1]
    calls = lax.axis_size(CALLS)
    pair = lax.axis_size("cc")
    spread = lax.axis_size(CALLS[:2])
    ring = lax.axis_size("cx")
    group = lax.axis_size("cy")
    ctx = ring * group
    block_rows = model_width // calls
    block_cols = grad_width // ctx
    col_factor = grad_all.reshape(frame_count, ring, group, block_cols).transpose(2, 0, 1, 3)
    col_factor = col_factor.reshape(group, frame_count, ring * block_cols)
    row_factor = jnp.broadcast_to(frame_rows[None], (group, frame_count, model_width))
    got_rows = lax.all_to_all(row_factor, "cy", 0, 0, tiled=True)
    got_cols = lax.all_to_all(col_factor, "cy", 0, 0, tiled=True)
    row_pieces = got_rows.reshape(group, frame_count, spread, pair, block_rows)
    col_pieces = got_cols.reshape(group, frame_count, ring, block_cols)
    core = lax.axis_index("cc")
    keep, send = [
        jnp.einsum(
            "sfna,sfxb->xnab",
            lax.dynamic_index_in_dim(row_pieces, h, 3, keepdims=False),
            col_pieces,
            preferred_element_type=jnp.float32,
        ).reshape(ring, spread, block_rows * block_cols)
        for h in (core, pair - 1 - core)
    ]
    half = keep + lax.ppermute(send, "cc", [(0, 1), (1, 0)])
    part = jnp.sum(lax.all_to_all(half, "cx", 0, 0, tiled=True), axis=0)
    summed = jnp.sum(lax.all_to_all(part, CALLS[:2], 0, 0, tiled=True), axis=0)
    return summed.reshape(block_rows, block_cols)


def body(frames_in, w_qkv, out_grad, lengths):
    frame_rows = frames_in[0]
    frame_count, model_width = frame_rows.shape
    inner_width = w_qkv.shape[1] // 3
    window = WIN
    offset = lax.axis_index(CTX) * frame_count
    length_now = lengths[0]
    qkv = jnp.dot(frame_rows, w_qkv, preferred_element_type=jnp.float32).astype(jnp.bfloat16)
    queries = qkv[:, :inner_width]
    key_value = with_halo(qkv[:, inner_width:], ((CTX, 0),), window)
    query_pos = offset + jnp.arange(frame_count, dtype=jnp.int32)
    key_pos = offset - window + jnp.arange(frame_count + 2 * window, dtype=jnp.int32)
    allowed = band_mask(query_pos, key_pos, length_now)
    live_rows = query_pos < length_now
    living = live_rows.astype(jnp.float32)
    cotangent = jnp.where(live_rows[:, None], out_grad[0], jnp.zeros_like(out_grad[0]))
    context, grad_query, grad_terms = attend(queries, key_value, cotangent, allowed, living)
    own_part = grad_terms[window : window + frame_count]
    rim_part = jnp.concatenate(
        [grad_terms[:window], grad_terms[window + frame_count :]], axis=0
    ).astype(jnp.bfloat16)
    returned = with_halo(rim_part, ((CTX, 0),), window)
    from_left = returned[:window].astype(jnp.float32)
    from_right = returned[3 * window :].astype(jnp.float32)
    summed = own_part + from_left
    summed = summed + from_right
    grad_kv = summed.astype(jnp.bfloat16)
    grad_all = jnp.concatenate([grad_query, grad_kv], axis=1)
    in_grad = lax.dot_general(
        grad_all, w_qkv, (((1,), (1,)), ((), ())), preferred_element_type=jnp.float32
    ).astype(jnp.bfloat16)
    weight_grad = weight_gradient(frame_rows, grad_all)
    return (context[None], in_grad[None], weight_grad)


def solution(mesh):
    calls, ctx = mesh.devices.shape
    pair = 2
    group = 4
    shape = (2, calls // (2 * pair), pair, ctx // group, group)
    fine = Mesh(mesh.devices.reshape(shape), CALLS + CTX)
    frames = P(CALLS, CTX, None)
    in_specs = (frames, P(), frames, P(CALLS))
    out_specs = (frames, frames, P(CALLS, CTX))
    return jax.shard_map(body, mesh=fine, in_specs=in_specs, out_specs=out_specs, check_vma=False)
```
